32 devices in a mesh: hours: 2 (over y), pair: 4 (over z), win: 2 (over x), band: 2 (over core).
Axes of the slice: x: 2, y: 2, z: 4, core: 2. Of those that a mesh axis runs over, the one named last changes fastest.
Arguments:
- records: bfloat16 [256, 3, 32, 512], P(('hours', 'win'), None, 'pair'), parts along dimension 0, may hold values from -180 to 180
- valid_mask: int32 [256, 32], P(('hours', 'win'), 'pair'), parts along dimension 0, may hold values from 0 to 1, as said below
- round_keys: int32 [4], replicated, may hold values from 0 to 3, as said below
Outputs:
- correlations: float32 [4, 64, 3, 24, 256], P(None, ('hours', 'pair', 'win', 'band')), parts along dimension 1
The draws below stay inside these ranges and needn't reach their ends.
There are 2 independent parts, one for each index of `hours`. The reference program is written for one: setup_inputs(seed, part) draws one part's arguments, and reference() takes and returns one part's arrays. A program takes and returns all parts, laid end to end along the dimension named above; an argument that names none is the same for every part. Nothing has to cross between parts.
Inputs may be any that keep to these rules, and one draw needn't show every extreme that they name: `valid_mask`: 1 where the window holds usable data at that station, else 0. `round_keys`: distinct; in round r every block p is paired with block p XOR round_keys[r], and 0 pairs a block with itself.
All inputs are finite; a program needn't handle non-finite values.
Results may differ from the reference program's by a relative error of at most 0.005.
Values may be sent and summed in bfloat16 or wider, within the bound.
No kernel may reach another device: no remote copies, remote signals or barrier semaphores. Data moves between devices by JAX's collectives and lax.ppermute only.
A program may use at most 192 MiB of HBM per device.

```python
import math
import jax
import jax.numpy as jnp
from jax import lax

NT = 512
FREQ = 128
NLAG = 256
SB = 8
ROUNDS = 4
BLOCKS = 4
STATIONS = 32
WINDOWS = 128


def draw_records(key, part):
    gain_key, level_key, noise_key = jax.random.split(key, 3)
    full_shape = (WINDOWS, 3, STATIONS, NT)
    station_gain = jnp.exp(jax.random.uniform(gain_key, (1, 3, STATIONS, 1), jnp.float32, 0.0, math.log(10.0)))
    levels = jnp.exp(jax.random.uniform(level_key, (WINDOWS, 1, STATIONS, 1), jnp.float32, 0.0, math.log(3.0)))
    values = jax.random.normal(noise_key, full_shape, jnp.float32)
    return (station_gain * levels * jnp.clip(values, -6.0, 6.0)).astype(jnp.bfloat16)


def draw_valid_mask(key, part):
    uptime_key, throw_key = jax.random.split(key, 2)
    uptime = jax.random.randint(uptime_key, (1, STATIONS), 1, 21, jnp.int32)
    window_rise = 6 + 14 * jnp.arange(WINDOWS, dtype=jnp.int32) // max(WINDOWS - 1, 1)
    throws = jax.random.randint(throw_key, (WINDOWS, STATIONS), 0, 400, jnp.int32)
    return (throws < uptime * window_rise[:, None]).astype(jnp.int32)


def draw_round_keys(key, part):
    return jax.random.permutation(key, BLOCKS)[:ROUNDS].astype(jnp.int32)


def setup_inputs(seed: int = 0, part: int = 0) -> dict:
    key_list = jax.random.split(jax.random.key(seed), 4)
    own_keys = jax.random.split(jax.random.fold_in(key_list[3], part), 4)
    records = draw_records(jax.random.fold_in(jax.random.fold_in(key_list[3], part), 71), part)
    valid_mask = draw_valid_mask(jax.random.fold_in(jax.random.fold_in(key_list[3], part), 71), part)
    round_keys = draw_round_keys(jax.random.fold_in(key_list[3], 71), part)
    return dict(records=records, valid_mask=valid_mask, round_keys=round_keys)


def dft_table(sample_points, bin_count, first_bin):
    sample_moments = jnp.arange(sample_points, dtype=jnp.int32)
    spectral_bin_index = first_bin + 1 + jnp.arange(bin_count, dtype=jnp.int32)
    phase_turns = jnp.mod(sample_moments[:, None] * spectral_bin_index[None, :], sample_points)
    phases = phase_turns.astype(jnp.float32) * (2.0 * math.pi / sample_points)
    hanning_taper = 0.5 - 0.5 * jnp.cos(sample_moments.astype(jnp.float32) * (2.0 * math.pi / sample_points))
    weight = (hanning_taper * math.sqrt(8.0 / (3.0 * sample_points)))[:, None]
    return jnp.concatenate([weight * jnp.cos(phases), -(weight * jnp.sin(phases))], axis=1).astype(jnp.bfloat16)

def lag_table(sample_points, bin_count, first_bin, lag_count, all_bins):
    spectral_bin_index = first_bin + 1 + jnp.arange(bin_count, dtype=jnp.int32)
    shifts = jnp.arange(lag_count, dtype=jnp.int32) - lag_count // 2
    phase_turns = jnp.mod(spectral_bin_index[:, None] * shifts[None, :], sample_points)
    phases = phase_turns.astype(jnp.float32) * (2.0 * math.pi / sample_points)
    lag_scale = 1.0 / math.sqrt(all_bins)
    return jnp.concatenate([jnp.cos(phases) * lag_scale, -(jnp.sin(phases) * lag_scale)], axis=0)

def whiten(spectra, validity):
    bin_count = spectra.shape[-1] // 2
    real_part = spectra[..., :bin_count]
    imag_part = spectra[..., bin_count:]
    band_power = lax.optimization_barrier(jnp.mean(real_part * real_part + imag_part * imag_part, axis=1))
    amplitude = jnp.sqrt(jnp.maximum(band_power, 0.25))
    factor = validity[:, :, None] / amplitude
    factor = jnp.concatenate([factor, factor], axis=-1)
    return (spectra * factor[:, None]).astype(jnp.bfloat16)

def cross_spectra(own_block, partner):
    window_count, comp_count, station_count, twice_values = own_block.shape
    bin_count = twice_values // 2
    lanes = jnp.arange(twice_values, dtype=jnp.int32)
    lower = lanes < bin_count
    signs = jnp.where(lower, -1.0, 1.0).astype(partner.dtype)
    turned = jnp.roll(partner, bin_count, axis=-1) * signs
    direct = jnp.einsum('waik,wbjk->iabjk', own_block, partner, preferred_element_type=jnp.float32)
    rotated = jnp.einsum('waik,wbjk->iabjk', own_block, turned, preferred_element_type=jnp.float32)
    real_both = direct + jnp.roll(direct, bin_count, axis=-1)
    imag_both = rotated + jnp.roll(rotated, bin_count, axis=-1)
    product = jnp.where(lower, real_both, imag_both)
    return product.reshape(station_count, comp_count, comp_count * station_count, twice_values)

def reference(records, valid_mask, round_keys):
    dft_rows = dft_table(NT, FREQ, 0)
    spectra = jnp.einsum('wcsn,nk->wcsk', records.astype(jnp.float32), dft_rows.astype(jnp.float32))
    validity = valid_mask.astype(jnp.float32)
    whitened = whiten(spectra, validity)
    blocks = whitened.astype(jnp.float32).reshape(WINDOWS, 3, BLOCKS, SB, 2 * FREQ).transpose(2, 0, 1, 3, 4)
    block_valid = validity.reshape(WINDOWS, BLOCKS, SB).transpose(1, 0, 2)
    lag_rows = lag_table(NT, FREQ, 0, NLAG, FREQ)
    block_ids = jnp.arange(BLOCKS, dtype=jnp.int32)
    results = []
    for round_index in range(ROUNDS):
        partners = jnp.bitwise_xor(block_ids, round_keys[round_index])
        pair_spectra = jax.vmap(cross_spectra)(blocks, blocks[partners])
        pair_counts = jnp.einsum('pwi,pwj->pij', block_valid, block_valid[partners])
        divisor = jnp.tile(jnp.maximum(pair_counts, 1.0), (1, 1, 3))
        stacked_result = pair_spectra / divisor[:, :, None, :, None]
        lagged = jnp.einsum('piayk,kl->piayl', stacked_result, lag_rows, precision=lax.Precision.HIGHEST)
        results.append(lagged.reshape(STATIONS, 3, 3 * SB, NLAG))
    return jnp.stack(results)
```

```python
import math

import jax
import jax.numpy as jnp
from jax import lax
from jax.sharding import PartitionSpec as P

FREQ = 128
NLAG = 256
ROUNDS = 4


def dft_table(sample_points, bin_count, first_bin):
    sample_moments = jnp.arange(sample_points, dtype=jnp.int32)
    spectral_bin_index = first_bin + 1 + jnp.arange(bin_count, dtype=jnp.int32)
    phase_turns = jnp.mod(sample_moments[:, None] * spectral_bin_index[None, :], sample_points)
    phases = phase_turns.astype(jnp.float32) * (2.0 * math.pi / sample_points)
    hanning_taper = 0.5 - 0.5 * jnp.cos(
        sample_moments.astype(jnp.float32) * (2.0 * math.pi / sample_points)
    )
    weight = (hanning_taper * math.sqrt(8.0 / (3.0 * sample_points)))[:, None]
    return jnp.concatenate([weight * jnp.cos(phases), -(weight * jnp.sin(phases))], axis=1).astype(
        jnp.bfloat16
    )


def lag_table(sample_points, bin_count, first_bin, lag_count, all_bins):
    spectral_bin_index = first_bin + 1 + jnp.arange(bin_count, dtype=jnp.int32)
    shifts = jnp.arange(lag_count, dtype=jnp.int32) - lag_count // 2
    phase_turns = jnp.mod(spectral_bin_index[:, None] * shifts[None, :], sample_points)
    phases = phase_turns.astype(jnp.float32) * (2.0 * math.pi / sample_points)
    lag_scale = 1.0 / math.sqrt(all_bins)
    return jnp.concatenate([jnp.cos(phases) * lag_scale, -(jnp.sin(phases) * lag_scale)], axis=0)


def whiten(spectra, validity):
    bin_count = spectra.shape[-1] // 2
    real_part = spectra[..., :bin_count]
    imag_part = spectra[..., bin_count:]
    band_power = jnp.mean(real_part * real_part + imag_part * imag_part, axis=1)
    amplitude = jnp.sqrt(jnp.maximum(band_power, 0.25))
    factor = validity[:, :, None] / amplitude
    factor = jnp.concatenate([factor, factor], axis=-1)
    return (spectra * factor[:, None]).astype(jnp.bfloat16)


def body(records, valid_mask, round_keys):
    window_count, comp_count, station_count, sample_points = records.shape
    bands = lax.axis_size("band")
    wins = lax.axis_size("win")
    band_index = lax.axis_index("band")
    win_index = lax.axis_index("win")
    pair_index = lax.axis_index("pair")
    nb = FREQ // bands
    rounds = round_keys.shape[0]

    mask_all = lax.all_gather(valid_mask, ("pair", "win"), axis=0, tiled=False)
    mask_all = mask_all.reshape(lax.axis_size("pair"), wins * window_count, station_count)

    dft_rows = dft_table(sample_points, nb, band_index * nb)
    spectra = jnp.einsum("wcsn,nk->wcsk", records, dft_rows, preferred_element_type=jnp.float32)
    validity = valid_mask.astype(jnp.float32)
    whitened = whiten(spectra, validity)

    gathered = lax.all_gather(whitened, "pair", axis=0, tiled=False)
    partner_list = jnp.bitwise_xor(pair_index, round_keys)
    partners = jnp.take(gathered, partner_list, axis=0, mode="clip")

    own = whitened.reshape(window_count, comp_count, station_count, 2, nb)
    other = partners.reshape(rounds, window_count, comp_count, station_count, 2, nb)
    prod = jnp.einsum(
        "waitf,rwbjuf->iarbjtuf", own, other, preferred_element_type=jnp.float32
    )
    real = prod[..., 0, 0, :] + prod[..., 1, 1, :]
    imag = prod[..., 1, 0, :] - prod[..., 0, 1, :]
    cross = jnp.stack([real, imag], axis=-2)

    summed = lax.psum_scatter(cross, "win", scatter_dimension=0, tiled=True)
    per_band = summed.shape[0] // bands
    summed = summed.reshape((bands, per_band) + summed.shape[1:])
    swapped = lax.all_to_all(summed, "band", split_axis=0, concat_axis=0, tiled=True)
    stacked = jnp.moveaxis(swapped, 0, -3)
    stacked = stacked.reshape(stacked.shape[:-3] + (bands * 2 * nb,))

    own_mask = mask_all[pair_index].astype(jnp.float32)
    first_row = (win_index * bands + band_index) * per_band
    own_mask = lax.dynamic_slice_in_dim(own_mask, first_row, per_band, axis=1)
    partner_mask = jnp.take(mask_all, partner_list, axis=0, mode="clip").astype(jnp.float32)
    counts = jnp.einsum("wi,rwj->irj", own_mask, partner_mask)
    divisor = jnp.maximum(counts, 1.0)[:, None, :, None, :, None]
    stacked = stacked / divisor

    full_lag = lag_table(sample_points, FREQ, 0, NLAG, FREQ)
    full_lag = full_lag.reshape(2, bands, nb, NLAG).transpose(1, 0, 2, 3).reshape(-1, NLAG)
    lagged = jnp.einsum(
        "iarbje,el->riabjl",
        stacked,
        full_lag,
        precision=lax.Precision.HIGHEST,
        preferred_element_type=jnp.float32,
    )
    return lagged.reshape(rounds, per_band, comp_count, comp_count * station_count, NLAG)


def solution(mesh):
    placed = (P(("hours", "win"), None, "pair", None), P(("hours", "win"), "pair"), P())
    return jax.shard_map(
        body,
        mesh=mesh,
        in_specs=placed,
        out_specs=P(None, ("hours", "pair", "win", "band"), None, None, None),
        check_vma=False,
    )
```

```python
import math

import jax
import jax.numpy as jnp
from jax import lax
from jax.sharding import PartitionSpec as P

FREQ = 128
NLAG = 256
ROUNDS = 4


def dft_table(sample_points, bin_count, first_bin):
    sample_moments = jnp.arange(sample_points, dtype=jnp.int32)
    spectral_bin_index = first_bin + 1 + jnp.arange(bin_count, dtype=jnp.int32)
    phase_turns = jnp.mod(sample_moments[:, None] * spectral_bin_index[None, :], sample_points)
    phases = phase_turns.astype(jnp.float32) * (2.0 * math.pi / sample_points)
    hanning_taper = 0.5 - 0.5 * jnp.cos(
        sample_moments.astype(jnp.float32) * (2.0 * math.pi / sample_points)
    )
    weight = (hanning_taper * math.sqrt(8.0 / (3.0 * sample_points)))[:, None]
    return jnp.concatenate([weight * jnp.cos(phases), -(weight * jnp.sin(phases))], axis=1).astype(
        jnp.bfloat16
    )


def lag_table(sample_points, bin_count, first_bin, lag_count, all_bins):
    spectral_bin_index = first_bin + 1 + jnp.arange(bin_count, dtype=jnp.int32)
    shifts = jnp.arange(lag_count, dtype=jnp.int32) - lag_count // 2
    phase_turns = jnp.mod(spectral_bin_index[:, None] * shifts[None, :], sample_points)
    phases = phase_turns.astype(jnp.float32) * (2.0 * math.pi / sample_points)
    lag_scale = 1.0 / math.sqrt(all_bins)
    return jnp.concatenate([jnp.cos(phases) * lag_scale, -(jnp.sin(phases) * lag_scale)], axis=0)


def whiten_t(spectra_t, validity_t):
    bin_count = spectra_t.shape[0] // 2
    real_part = spectra_t[:bin_count]
    imag_part = spectra_t[bin_count:]
    band_power = jnp.mean(real_part * real_part + imag_part * imag_part, axis=1)
    amplitude = jnp.sqrt(jnp.maximum(band_power, 0.25))
    factor = validity_t[None] / amplitude
    split = spectra_t.reshape((2, bin_count) + spectra_t.shape[1:])
    return (split * factor[None, :, None]).astype(jnp.bfloat16)


def body(records, valid_mask, round_keys):
    window_count, comp_count, station_count, sample_points = records.shape
    bands = lax.axis_size("band")
    band_index = lax.axis_index("band")
    pair_index = lax.axis_index("pair")
    nb = FREQ // bands
    rounds = round_keys.shape[0]
    rows = 2 * comp_count * station_count

    dft_rows = dft_table(sample_points, nb, band_index * nb)
    spectra_t = jnp.einsum("wcsn,nk->kcsw", records, dft_rows, preferred_element_type=jnp.float32)
    validity_t = valid_mask.astype(jnp.float32).T
    whitened = whiten_t(spectra_t, validity_t)
    own = whitened.transpose(1, 0, 2, 3, 4).reshape(nb, rows, window_count)

    vslab = jnp.zeros((1, rows, window_count), jnp.bfloat16)
    vslab = vslab.at[0, :station_count].set(validity_t.astype(jnp.bfloat16))
    payload = jnp.concatenate([own, vslab], axis=0)

    gathered = lax.all_gather(payload, "pair", axis=0, tiled=False)
    partner_list = jnp.bitwise_xor(pair_index, round_keys)
    partners = jnp.take(gathered, partner_list, axis=0, mode="clip")
    partner_valid = partners[:, nb, :station_count, :].astype(jnp.float32)
    rhs = partners[:, :nb].transpose(1, 0, 2, 3).reshape(nb, rounds * rows, window_count)

    prod = jnp.einsum("fxw,fyw->fxy", own, rhs, preferred_element_type=jnp.float32)
    prod = prod.reshape(nb, 2, comp_count, station_count, rounds, 2, comp_count, station_count)
    real = prod[:, 0, :, :, :, 0] + prod[:, 1, :, :, :, 1]
    imag = prod[:, 1, :, :, :, 0] - prod[:, 0, :, :, :, 1]
    cross = jnp.stack([real, imag], axis=0)
    cross = cross.transpose(3, 2, 4, 5, 6, 0, 1)
    per_station = comp_count * rounds * comp_count * station_count
    cross = cross.reshape(station_count, per_station, 2 * nb)

    counts = jnp.einsum("iw,rjw->irj", validity_t, partner_valid)
    counts = counts.reshape(station_count, 1, rounds * station_count)
    counts = jnp.pad(counts, ((0, 0), (0, 0), (0, 2 * nb - rounds * station_count)))
    ext = jnp.concatenate([cross, counts], axis=1)

    summed = lax.psum_scatter(ext, "win", scatter_dimension=0, tiled=True)
    per_band = summed.shape[0] // bands
    summed = summed.reshape((bands, per_band) + summed.shape[1:])
    swapped = lax.all_to_all(summed, "band", split_axis=0, concat_axis=0, tiled=True)
    totals = swapped[0, :, per_station, : rounds * station_count]
    totals = totals.reshape(per_band, 1, rounds, 1, station_count, 1)
    spec = swapped[:, :, :per_station, :].transpose(1, 2, 0, 3)
    spec = spec.reshape(per_band, comp_count, rounds, comp_count, station_count, bands * 2 * nb)
    stacked = spec / jnp.maximum(totals, 1.0)

    full_lag = lag_table(sample_points, FREQ, 0, NLAG, FREQ)
    full_lag = full_lag.reshape(2, bands, nb, NLAG).transpose(1, 0, 2, 3).reshape(-1, NLAG)
    lagged = jnp.einsum(
        "iarbje,el->riabjl",
        stacked,
        full_lag,
        precision=lax.Precision.HIGHEST,
        preferred_element_type=jnp.float32,
    )
    return lagged.reshape(rounds, per_band, comp_count, comp_count * station_count, NLAG)


def solution(mesh):
    placed = (P(("hours", "win"), None, "pair", None), P(("hours", "win"), "pair"), P())
    return jax.shard_map(
        body,
        mesh=mesh,
        in_specs=placed,
        out_specs=P(None, ("hours", "pair", "win", "band"), None, None, None),
        check_vma=False,
    )
```

```python
import math

import jax
import jax.numpy as jnp
from jax import lax
from jax.sharding import PartitionSpec as P

FREQ = 128
NLAG = 256
ROUNDS = 4


def dft_table(sample_points, bin_count, first_bin):
    sample_moments = jnp.arange(sample_points, dtype=jnp.int32)
    spectral_bin_index = first_bin + 1 + jnp.arange(bin_count, dtype=jnp.int32)
    phase_turns = jnp.mod(sample_moments[:, None] * spectral_bin_index[None, :], sample_points)
    phases = phase_turns.astype(jnp.float32) * (2.0 * math.pi / sample_points)
    hanning_taper = 0.5 - 0.5 * jnp.cos(
        sample_moments.astype(jnp.float32) * (2.0 * math.pi / sample_points)
    )
    weight = (hanning_taper * math.sqrt(8.0 / (3.0 * sample_points)))[:, None]
    return jnp.concatenate([weight * jnp.cos(phases), -(weight * jnp.sin(phases))], axis=1).astype(
        jnp.bfloat16
    )


def lag_table(sample_points, bin_count, first_bin, lag_count, all_bins):
    spectral_bin_index = first_bin + 1 + jnp.arange(bin_count, dtype=jnp.int32)
    shifts = jnp.arange(lag_count, dtype=jnp.int32) - lag_count // 2
    phase_turns = jnp.mod(spectral_bin_index[:, None] * shifts[None, :], sample_points)
    phases = phase_turns.astype(jnp.float32) * (2.0 * math.pi / sample_points)
    lag_scale = 1.0 / math.sqrt(all_bins)
    return jnp.concatenate([jnp.cos(phases) * lag_scale, -(jnp.sin(phases) * lag_scale)], axis=0)


def whiten(spectra, validity):
    bin_count = spectra.shape[-1] // 2
    real_part = spectra[..., :bin_count]
    imag_part = spectra[..., bin_count:]
    band_power = jnp.mean(real_part * real_part + imag_part * imag_part, axis=1)
    amplitude = jnp.sqrt(jnp.maximum(band_power, 0.25))
    factor = validity[:, :, None] / amplitude
    factor = jnp.concatenate([factor, factor], axis=-1)
    return (spectra * factor[:, None]).astype(jnp.bfloat16)


def body(records, valid_mask, round_keys):
    window_count, comp_count, station_count, sample_points = records.shape
    bands = lax.axis_size("band")
    band_index = lax.axis_index("band")
    pair_index = lax.axis_index("pair")
    nb = FREQ // bands
    lanes = 2 * nb
    rounds = round_keys.shape[0]
    rows = window_count * comp_count * station_count
    half = nb // 2

    dft_rows = dft_table(sample_points, nb, band_index * nb)
    spectra = jnp.einsum("wcsn,nk->wcsk", records, dft_rows, preferred_element_type=jnp.float32)
    validity = valid_mask.astype(jnp.float32)
    whitened = whiten(spectra, validity).reshape(rows, lanes)

    vrows = -(-window_count * station_count // lanes)
    vflat = validity.astype(jnp.bfloat16).reshape(-1)
    vflat = jnp.pad(vflat, (0, vrows * lanes - vflat.shape[0])).reshape(vrows, lanes)
    payload = jnp.concatenate([whitened, vflat], axis=0)

    gathered = lax.all_gather(payload, "pair", axis=0, tiled=False)
    partner_list = jnp.bitwise_xor(pair_index, round_keys)
    partners = jnp.take(gathered, partner_list, axis=0, mode="clip")
    partner_valid = partners[:, rows:].reshape(rounds, -1)[:, : window_count * station_count]
    partner_valid = partner_valid.reshape(rounds, window_count, station_count).astype(jnp.float32)

    spec = partners[:, :rows].reshape(
        rounds, window_count, comp_count, station_count, 2, half, 2
    )
    rhs = spec.transpose(5, 0, 4, 2, 3, 6, 1).reshape(half, rounds * 2 * comp_count * station_count, 2 * window_count)
    mine = whitened.reshape(window_count, comp_count, station_count, 2, half, 2)
    mine = mine.transpose(4, 5, 3, 1, 2, 0)
    parity = jnp.arange(2)
    pick = (parity[:, None] == parity[None, :]).astype(jnp.bfloat16)
    lhs = mine[:, :, :, :, :, None, :] * pick[None, :, None, None, None, :, None]
    lhs = lhs.reshape(half, 2 * 2 * comp_count * station_count, 2 * window_count)

    prod = jnp.einsum("gxk,gyk->gxy", lhs, rhs, preferred_element_type=jnp.float32)
    prod = prod.reshape(half, 2, 2, comp_count, station_count, rounds, 2, comp_count, station_count)
    real = prod[:, :, 0, :, :, :, 0] + prod[:, :, 1, :, :, :, 1]
    imag = prod[:, :, 1, :, :, :, 0] - prod[:, :, 0, :, :, :, 1]
    cross = jnp.stack([real, imag], axis=0)
    cross = cross.transpose(4, 3, 5, 6, 7, 0, 1, 2)
    per_station = comp_count * rounds * comp_count * station_count
    cross = cross.reshape(station_count, per_station, lanes)

    counts = jnp.einsum("wi,rwj->irj", validity, partner_valid)
    counts = counts.reshape(station_count, 1, rounds * station_count)
    counts = jnp.pad(counts, ((0, 0), (0, 0), (0, lanes - rounds * station_count)))
    ext = jnp.concatenate([cross, counts], axis=1)

    summed = lax.psum_scatter(ext, "win", scatter_dimension=0, tiled=True)
    per_band = summed.shape[0] // bands
    summed = summed.reshape((bands, per_band) + summed.shape[1:])
    swapped = lax.all_to_all(summed, "band", split_axis=0, concat_axis=0, tiled=True)
    totals = swapped[0, :, per_station, : rounds * station_count]
    totals = totals.reshape(per_band, 1, rounds, 1, station_count, 1)
    spec = swapped[:, :, :per_station, :].transpose(1, 2, 0, 3)
    spec = spec.reshape(per_band, comp_count, rounds, comp_count, station_count, bands * lanes)
    stacked = spec / jnp.maximum(totals, 1.0)

    full_lag = lag_table(sample_points, FREQ, 0, NLAG, FREQ)
    full_lag = full_lag.reshape(2, bands, nb, NLAG).transpose(1, 0, 2, 3).reshape(-1, NLAG)
    lagged = jnp.einsum(
        "iarbje,el->riabjl",
        stacked,
        full_lag,
        precision=lax.Precision.HIGHEST,
        preferred_element_type=jnp.float32,
    )
    return lagged.reshape(rounds, per_band, comp_count, comp_count * station_count, NLAG)


def solution(mesh):
    placed = (P(("hours", "win"), None, "pair", None), P(("hours", "win"), "pair"), P())
    return jax.shard_map(
        body,
        mesh=mesh,
        in_specs=placed,
        out_specs=P(None, ("hours", "pair", "win", "band"), None, None, None),
        check_vma=False,
    )
```

```python
import math

import jax
import jax.numpy as jnp
from jax import lax
from jax.experimental import pallas as pl
from jax.experimental.pallas import tpu as pltpu
from jax.sharding import PartitionSpec as P

FREQ = 128
NLAG = 256
ROUNDS = 4


def dft_table(sample_points, bin_count, first_bin):
    sample_moments = jnp.arange(sample_points, dtype=jnp.int32)
    spectral_bin_index = first_bin + 1 + jnp.arange(bin_count, dtype=jnp.int32)
    phase_turns = jnp.mod(sample_moments[:, None] * spectral_bin_index[None, :], sample_points)
    phases = phase_turns.astype(jnp.float32) * (2.0 * math.pi / sample_points)
    hanning_taper = 0.5 - 0.5 * jnp.cos(
        sample_moments.astype(jnp.float32) * (2.0 * math.pi / sample_points)
    )
    weight = (hanning_taper * math.sqrt(8.0 / (3.0 * sample_points)))[:, None]
    return jnp.concatenate([weight * jnp.cos(phases), -(weight * jnp.sin(phases))], axis=1).astype(
        jnp.bfloat16
    )


def lag_table(sample_points, bin_count, first_bin, lag_count, all_bins):
    spectral_bin_index = first_bin + 1 + jnp.arange(bin_count, dtype=jnp.int32)
    shifts = jnp.arange(lag_count, dtype=jnp.int32) - lag_count // 2
    phase_turns = jnp.mod(spectral_bin_index[:, None] * shifts[None, :], sample_points)
    phases = phase_turns.astype(jnp.float32) * (2.0 * math.pi / sample_points)
    lag_scale = 1.0 / math.sqrt(all_bins)
    return jnp.concatenate([jnp.cos(phases) * lag_scale, -(jnp.sin(phases) * lag_scale)], axis=0)


def whiten(spectra, validity):
    bin_count = spectra.shape[-1] // 2
    real_part = spectra[..., :bin_count]
    imag_part = spectra[..., bin_count:]
    band_power = jnp.mean(real_part * real_part + imag_part * imag_part, axis=1)
    amplitude = jnp.sqrt(jnp.maximum(band_power, 0.25))
    factor = validity[:, :, None] / amplitude
    factor = jnp.concatenate([factor, factor], axis=-1)
    return (spectra * factor[:, None]).astype(jnp.bfloat16)


def cross_kernel(own_ref, part_ref, out_ref):
    window_count = own_ref.shape[0]
    station_count = own_ref.shape[2]
    lanes = own_ref.shape[3]
    nb = lanes // 2
    lower = lax.broadcasted_iota(jnp.int32, (station_count, station_count, lanes), 2) < nb
    for b in range(part_ref.shape[2]):

        def step(w, carry):
            direct, turned = carry
            a_rows = own_ref[w, 0]
            b_rows = part_ref[0, w, b]
            b_turn = pltpu.roll(b_rows, nb, 1)
            direct = direct + a_rows[:, None, :] * b_rows[None, :, :]
            turned = turned + a_rows[:, None, :] * b_turn[None, :, :]
            return direct, turned

        zero = jnp.zeros((station_count, station_count, lanes), jnp.float32)
        direct, turned = lax.fori_loop(0, window_count, step, (zero, zero), unroll=4)
        real = direct + pltpu.roll(direct, nb, 2)
        imag = turned - pltpu.roll(turned, nb, 2)
        out_ref[:, 0, 0, b] = jnp.where(lower, real, imag)


def cross_products(own, partners):
    rounds, window_count, comp_count, station_count, lanes = partners.shape
    flops = 4 * rounds * window_count * comp_count * comp_count * station_count * station_count * lanes
    return pl.pallas_call(
        cross_kernel,
        grid=(comp_count, rounds),
        in_specs=[
            pl.BlockSpec((window_count, 1, station_count, lanes), lambda a, r: (0, a, 0, 0)),
            pl.BlockSpec(
                (1, window_count, comp_count, station_count, lanes), lambda a, r: (r, 0, 0, 0, 0)
            ),
        ],
        out_specs=pl.BlockSpec(
            (station_count, 1, 1, comp_count, station_count, lanes),
            lambda a, r: (0, a, r, 0, 0, 0),
        ),
        out_shape=jax.ShapeDtypeStruct(
            (station_count, comp_count, rounds, comp_count, station_count, lanes), jnp.float32
        ),
        cost_estimate=pl.CostEstimate(
            flops=flops,
            transcendentals=0,
            bytes_accessed=4 * (own.size * rounds + partners.size + station_count * comp_count * rounds * comp_count * station_count * lanes),
        ),
    )(own, partners)


def body(records, valid_mask, round_keys):
    window_count, comp_count, station_count, sample_points = records.shape
    bands = lax.axis_size("band")
    band_index = lax.axis_index("band")
    pair_index = lax.axis_index("pair")
    nb = FREQ // bands
    lanes = 2 * nb
    rounds = round_keys.shape[0]
    rows = window_count * comp_count * station_count

    dft_rows = dft_table(sample_points, nb, band_index * nb)
    spectra = jnp.einsum("wcsn,nk->wcsk", records, dft_rows, preferred_element_type=jnp.float32)
    validity = valid_mask.astype(jnp.float32)
    whitened = whiten(spectra, validity)

    vrows = -(-window_count * station_count // lanes)
    vflat = validity.astype(jnp.bfloat16).reshape(-1)
    vflat = jnp.pad(vflat, (0, vrows * lanes - vflat.shape[0])).reshape(vrows, lanes)
    payload = jnp.concatenate([whitened.reshape(rows, lanes), vflat], axis=0)

    gathered = lax.all_gather(payload, "pair", axis=0, tiled=False)
    partner_list = jnp.bitwise_xor(pair_index, round_keys)
    partners = jnp.take(gathered, partner_list, axis=0, mode="clip")
    partner_valid = partners[:, rows:].reshape(rounds, -1)[:, : window_count * station_count]
    partner_valid = partner_valid.reshape(rounds, window_count, station_count).astype(jnp.float32)
    partner_spec = partners[:, :rows].astype(jnp.float32).reshape(
        rounds, window_count, comp_count, station_count, lanes
    )

    cross = cross_products(whitened.astype(jnp.float32), partner_spec)
    per_station = comp_count * rounds * comp_count * station_count
    cross = cross.reshape(station_count, per_station, lanes)

    counts = jnp.einsum("wi,rwj->irj", validity, partner_valid)
    counts = counts.reshape(station_count, 1, rounds * station_count)
    counts = jnp.pad(counts, ((0, 0), (0, 0), (0, lanes - rounds * station_count)))
    ext = jnp.concatenate([cross, counts], axis=1)

    summed = lax.psum_scatter(ext, "win", scatter_dimension=0, tiled=True)
    per_band = summed.shape[0] // bands
    summed = summed.reshape((bands, per_band) + summed.shape[1:])
    swapped = lax.all_to_all(summed, "band", split_axis=0, concat_axis=0, tiled=True)
    totals = swapped[0, :, per_station, : rounds * station_count]
    totals = totals.reshape(per_band, 1, rounds, 1, station_count, 1)
    spec = swapped[:, :, :per_station, :].transpose(1, 2, 0, 3)
    spec = spec.reshape(per_band, comp_count, rounds, comp_count, station_count, bands * lanes)
    stacked = spec / jnp.maximum(totals, 1.0)

    full_lag = lag_table(sample_points, FREQ, 0, NLAG, FREQ)
    full_lag = full_lag.reshape(2, bands, nb, NLAG).transpose(1, 0, 2, 3).reshape(-1, NLAG)
    lagged = jnp.einsum(
        "iarbje,el->riabjl",
        stacked,
        full_lag,
        precision=lax.Precision.HIGHEST,
        preferred_element_type=jnp.float32,
    )
    return lagged.reshape(rounds, per_band, comp_count, comp_count * station_count, NLAG)


def solution(mesh):
    placed = (P(("hours", "win"), None, "pair", None), P(("hours", "win"), "pair"), P())
    return jax.shard_map(
        body,
        mesh=mesh,
        in_specs=placed,
        out_specs=P(None, ("hours", "pair", "win", "band"), None, None, None),
        check_vma=False,
    )
```

```python
import math

import jax
import jax.numpy as jnp
from jax import lax
from jax.experimental import pallas as pl
from jax.experimental.pallas import tpu as pltpu
from jax.sharding import PartitionSpec as P

FREQ = 128
NLAG = 256
ROUNDS = 4


def dft_table(sample_points, bin_count, first_bin):
    sample_moments = jnp.arange(sample_points, dtype=jnp.int32)
    spectral_bin_index = first_bin + 1 + jnp.arange(bin_count, dtype=jnp.int32)
    phase_turns = jnp.mod(sample_moments[:, None] * spectral_bin_index[None, :], sample_points)
    phases = phase_turns.astype(jnp.float32) * (2.0 * math.pi / sample_points)
    hanning_taper = 0.5 - 0.5 * jnp.cos(
        sample_moments.astype(jnp.float32) * (2.0 * math.pi / sample_points)
    )
    weight = (hanning_taper * math.sqrt(8.0 / (3.0 * sample_points)))[:, None]
    return jnp.concatenate([weight * jnp.cos(phases), -(weight * jnp.sin(phases))], axis=1).astype(
        jnp.bfloat16
    )


def lag_table(sample_points, bin_count, first_bin, lag_count, all_bins):
    spectral_bin_index = first_bin + 1 + jnp.arange(bin_count, dtype=jnp.int32)
    shifts = jnp.arange(lag_count, dtype=jnp.int32) - lag_count // 2
    phase_turns = jnp.mod(spectral_bin_index[:, None] * shifts[None, :], sample_points)
    phases = phase_turns.astype(jnp.float32) * (2.0 * math.pi / sample_points)
    lag_scale = 1.0 / math.sqrt(all_bins)
    return jnp.concatenate([jnp.cos(phases) * lag_scale, -(jnp.sin(phases) * lag_scale)], axis=0)


def whiten(spectra, validity):
    bin_count = spectra.shape[-1] // 2
    real_part = spectra[..., :bin_count]
    imag_part = spectra[..., bin_count:]
    band_power = jnp.mean(real_part * real_part + imag_part * imag_part, axis=1)
    amplitude = jnp.sqrt(jnp.maximum(band_power, 0.25))
    factor = validity[:, :, None] / amplitude
    factor = jnp.concatenate([factor, factor], axis=-1)
    return (spectra * factor[:, None]).astype(jnp.bfloat16)


def cross_kernel(own_ref, part_ref, out_ref):
    window_count = own_ref.shape[0]
    station_count = own_ref.shape[2]
    lanes = own_ref.shape[4]
    nb = lanes // 2
    lower = lax.broadcasted_iota(jnp.int32, (station_count, station_count, lanes), 2) < nb
    for b in range(part_ref.shape[2]):

        def step(w, carry):
            direct, turned = carry
            a_rows = own_ref[w, 0]
            b_rows = part_ref[0, w, b]
            b_turn = pltpu.roll(b_rows, nb, 1)
            direct = direct + a_rows * b_rows[None, :, :]
            turned = turned + a_rows * b_turn[None, :, :]
            return direct, turned

        zero = jnp.zeros((station_count, station_count, lanes), jnp.float32)
        direct, turned = lax.fori_loop(0, window_count, step, (zero, zero), unroll=4)
        real = direct + pltpu.roll(direct, nb, 2)
        imag = turned - pltpu.roll(turned, nb, 2)
        out_ref[:, 0, 0, b] = jnp.where(lower, real, imag)


def cross_products(own, partners):
    rounds, window_count, comp_count, station_count, lanes = partners.shape
    own = jnp.broadcast_to(own[:, :, :, None, :], (window_count, comp_count, station_count, station_count, lanes))
    flops = 4 * rounds * window_count * comp_count * comp_count * station_count * station_count * lanes
    return pl.pallas_call(
        cross_kernel,
        grid=(comp_count, rounds),
        in_specs=[
            pl.BlockSpec(
                (window_count, 1, station_count, station_count, lanes), lambda a, r: (0, a, 0, 0, 0)
            ),
            pl.BlockSpec(
                (1, window_count, comp_count, station_count, lanes), lambda a, r: (r, 0, 0, 0, 0)
            ),
        ],
        out_specs=pl.BlockSpec(
            (station_count, 1, 1, comp_count, station_count, lanes),
            lambda a, r: (0, a, r, 0, 0, 0),
        ),
        out_shape=jax.ShapeDtypeStruct(
            (station_count, comp_count, rounds, comp_count, station_count, lanes), jnp.float32
        ),
        cost_estimate=pl.CostEstimate(
            flops=flops,
            transcendentals=0,
            bytes_accessed=4 * (own.size + partners.size + station_count * comp_count * rounds * comp_count * station_count * lanes),
        ),
    )(own, partners)


def body(records, valid_mask, round_keys):
    window_count, comp_count, station_count, sample_points = records.shape
    bands = lax.axis_size("band")
    band_index = lax.axis_index("band")
    pair_index = lax.axis_index("pair")
    nb = FREQ // bands
    lanes = 2 * nb
    rounds = round_keys.shape[0]
    rows = window_count * comp_count * station_count

    dft_rows = dft_table(sample_points, nb, band_index * nb)
    spectra = jnp.einsum("wcsn,nk->wcsk", records, dft_rows, preferred_element_type=jnp.float32)
    validity = valid_mask.astype(jnp.float32)
    whitened = whiten(spectra, validity)

    vrows = -(-window_count * station_count // lanes)
    vflat = validity.astype(jnp.bfloat16).reshape(-1)
    vflat = jnp.pad(vflat, (0, vrows * lanes - vflat.shape[0])).reshape(vrows, lanes)
    payload = jnp.concatenate([whitened.reshape(rows, lanes), vflat], axis=0)

    gathered = lax.all_gather(payload, "pair", axis=0, tiled=False)
    partner_list = jnp.bitwise_xor(pair_index, round_keys)
    partners = jnp.take(gathered, partner_list, axis=0, mode="clip")
    partner_valid = partners[:, rows:].reshape(rounds, -1)[:, : window_count * station_count]
    partner_valid = partner_valid.reshape(rounds, window_count, station_count).astype(jnp.float32)
    partner_spec = partners[:, :rows].astype(jnp.float32).reshape(
        rounds, window_count, comp_count, station_count, lanes
    )

    cross = cross_products(whitened.astype(jnp.float32), partner_spec)
    per_station = comp_count * rounds * comp_count * station_count
    cross = cross.reshape(station_count, per_station, lanes)

    counts = jnp.einsum("wi,rwj->irj", validity, partner_valid)
    counts = counts.reshape(station_count, 1, rounds * station_count)
    counts = jnp.pad(counts, ((0, 0), (0, 0), (0, lanes - rounds * station_count)))
    ext = jnp.concatenate([cross, counts], axis=1)

    wins = lax.axis_size("win")
    if wins == 2 and bands == 2:
        per_band = station_count // (wins * bands)
        me = lax.axis_index("win") * bands + band_index
        pieces = []
        for flip in range(wins * bands):
            chunk = lax.dynamic_slice_in_dim(ext, (me ^ flip) * per_band, per_band, 0)
            if flip:
                perm = [(k, k ^ flip) for k in range(wins * bands)]
                chunk = lax.ppermute(chunk, ("win", "band"), perm)
            pieces.append(chunk)
        same = pieces[0] + pieces[2]
        other = pieces[1] + pieces[3]
        first = jnp.where(band_index == 0, same, other)
        second = jnp.where(band_index == 0, other, same)
        swapped = jnp.stack([first, second], axis=0)
        totals = same[:, per_station, : rounds * station_count]
    else:
        summed = lax.psum_scatter(ext, "win", scatter_dimension=0, tiled=True)
        per_band = summed.shape[0] // bands
        summed = summed.reshape((bands, per_band) + summed.shape[1:])
        swapped = lax.all_to_all(summed, "band", split_axis=0, concat_axis=0, tiled=True)
        totals = swapped[0, :, per_station, : rounds * station_count]
    totals = totals.reshape(per_band, 1, rounds, 1, station_count, 1)
    spec = swapped[:bands, :, :per_station, :].transpose(1, 2, 0, 3)
    spec = spec.reshape(per_band, comp_count, rounds, comp_count, station_count, bands * lanes)
    stacked = spec / jnp.maximum(totals, 1.0)

    full_lag = lag_table(sample_points, FREQ, 0, NLAG, FREQ)
    full_lag = full_lag.reshape(2, bands, nb, NLAG).transpose(1, 0, 2, 3).reshape(-1, NLAG)
    lagged = jnp.einsum(
        "iarbje,el->riabjl",
        stacked,
        full_lag,
        precision=lax.Precision.HIGHEST,
        preferred_element_type=jnp.float32,
    )
    return lagged.reshape(rounds, per_band, comp_count, comp_count * station_count, NLAG)


def solution(mesh):
    placed = (P(("hours", "win"), None, "pair", None), P(("hours", "win"), "pair"), P())
    return jax.shard_map(
        body,
        mesh=mesh,
        in_specs=placed,
        out_specs=P(None, ("hours", "pair", "win", "band"), None, None, None),
        check_vma=False,
    )
```

```python
import math

import jax
import jax.numpy as jnp
from jax import lax
from jax.experimental import pallas as pl
from jax.experimental.pallas import tpu as pltpu
from jax.sharding import PartitionSpec as P

FREQ = 128
NLAG = 256
ROUNDS = 4
WSTEP = 4


def dft_table(sample_points, bin_count, first_bin):
    sample_moments = jnp.arange(sample_points, dtype=jnp.int32)
    spectral_bin_index = first_bin + 1 + jnp.arange(bin_count, dtype=jnp.int32)
    phase_turns = jnp.mod(sample_moments[:, None] * spectral_bin_index[None, :], sample_points)
    phases = phase_turns.astype(jnp.float32) * (2.0 * math.pi / sample_points)
    hanning_taper = 0.5 - 0.5 * jnp.cos(
        sample_moments.astype(jnp.float32) * (2.0 * math.pi / sample_points)
    )
    weight = (hanning_taper * math.sqrt(8.0 / (3.0 * sample_points)))[:, None]
    return jnp.concatenate([weight * jnp.cos(phases), -(weight * jnp.sin(phases))], axis=1).astype(
        jnp.bfloat16
    )


def lag_table(sample_points, bin_count, first_bin, lag_count, all_bins):
    spectral_bin_index = first_bin + 1 + jnp.arange(bin_count, dtype=jnp.int32)
    shifts = jnp.arange(lag_count, dtype=jnp.int32) - lag_count // 2
    phase_turns = jnp.mod(spectral_bin_index[:, None] * shifts[None, :], sample_points)
    phases = phase_turns.astype(jnp.float32) * (2.0 * math.pi / sample_points)
    lag_scale = 1.0 / math.sqrt(all_bins)
    return jnp.concatenate([jnp.cos(phases) * lag_scale, -(jnp.sin(phases) * lag_scale)], axis=0)


def whiten(spectra, validity):
    bin_count = spectra.shape[-1] // 2
    real_part = spectra[..., :bin_count]
    imag_part = spectra[..., bin_count:]
    band_power = jnp.mean(real_part * real_part + imag_part * imag_part, axis=1)
    amplitude = jnp.sqrt(jnp.maximum(band_power, 0.25))
    factor = validity[:, :, None] / amplitude
    factor = jnp.concatenate([factor, factor], axis=-1)
    return (spectra * factor[:, None]).astype(jnp.bfloat16)


def cross_kernel(own_ref, part_ref, out_ref):
    window_count = own_ref.shape[0]
    station_count = own_ref.shape[2]
    lanes = own_ref.shape[4]
    nb = lanes // 2
    lower = lax.broadcasted_iota(jnp.int32, (station_count, station_count, lanes), 2) < nb
    for b in range(part_ref.shape[2]):

        def step(k, carry):
            direct, turned = carry
            for u in range(WSTEP):
                w = k * WSTEP + u
                a_rows = own_ref[w, 0]
                b_rows = part_ref[0, w, b]
                b_turn = pltpu.roll(b_rows, nb, 1)
                direct = direct + a_rows * b_rows[None, :, :]
                turned = turned + a_rows * b_turn[None, :, :]
            return direct, turned

        zero = jnp.zeros((station_count, station_count, lanes), jnp.float32)
        direct, turned = lax.fori_loop(0, window_count // WSTEP, step, (zero, zero))
        real = direct + pltpu.roll(direct, nb, 2)
        imag = turned - pltpu.roll(turned, nb, 2)
        out_ref[:, 0, 0, b] = jnp.where(lower, real, imag)


def cross_products(own, partners):
    rounds, window_count, comp_count, station_count, lanes = partners.shape
    own = jnp.broadcast_to(own[:, :, :, None, :], (window_count, comp_count, station_count, station_count, lanes))
    flops = 4 * rounds * window_count * comp_count * comp_count * station_count * station_count * lanes
    return pl.pallas_call(
        cross_kernel,
        grid=(comp_count, rounds),
        in_specs=[
            pl.BlockSpec(
                (window_count, 1, station_count, station_count, lanes), lambda a, r: (0, a, 0, 0, 0)
            ),
            pl.BlockSpec(
                (1, window_count, comp_count, station_count, lanes), lambda a, r: (r, 0, 0, 0, 0)
            ),
        ],
        out_specs=pl.BlockSpec(
            (station_count, 1, 1, comp_count, station_count, lanes),
            lambda a, r: (0, a, r, 0, 0, 0),
        ),
        out_shape=jax.ShapeDtypeStruct(
            (station_count, comp_count, rounds, comp_count, station_count, lanes), jnp.float32
        ),
        cost_estimate=pl.CostEstimate(
            flops=flops,
            transcendentals=0,
            bytes_accessed=4 * (own.size + partners.size + station_count * comp_count * rounds * comp_count * station_count * lanes),
        ),
    )(own, partners)


def body(records, valid_mask, round_keys):
    window_count, comp_count, station_count, sample_points = records.shape
    bands = lax.axis_size("band")
    band_index = lax.axis_index("band")
    pair_index = lax.axis_index("pair")
    nb = FREQ // bands
    lanes = 2 * nb
    rounds = round_keys.shape[0]
    rows = window_count * comp_count * station_count

    dft_rows = dft_table(sample_points, nb, band_index * nb)
    spectra = jnp.einsum("wcsn,nk->wcsk", records, dft_rows, preferred_element_type=jnp.float32)
    validity = valid_mask.astype(jnp.float32)
    whitened = whiten(spectra, validity)

    vrows = -(-window_count * station_count // lanes)
    vflat = validity.astype(jnp.bfloat16).reshape(-1)
    vflat = jnp.pad(vflat, (0, vrows * lanes - vflat.shape[0])).reshape(vrows, lanes)
    payload = jnp.concatenate([whitened.reshape(rows, lanes), vflat], axis=0)

    gathered = lax.all_gather(payload, "pair", axis=0, tiled=False)
    partner_list = jnp.bitwise_xor(pair_index, round_keys)
    partners = jnp.take(gathered, partner_list, axis=0, mode="clip")
    partner_valid = partners[:, rows:].reshape(rounds, -1)[:, : window_count * station_count]
    partner_valid = partner_valid.reshape(rounds, window_count, station_count).astype(jnp.float32)
    partner_spec = partners[:, :rows].astype(jnp.float32).reshape(
        rounds, window_count, comp_count, station_count, lanes
    )

    cross = cross_products(whitened.astype(jnp.float32), partner_spec)
    per_station = comp_count * rounds * comp_count * station_count
    cross = cross.reshape(station_count, per_station, lanes)

    counts = jnp.einsum("wi,rwj->irj", validity, partner_valid)
    counts = counts.reshape(station_count, 1, rounds * station_count)
    counts = jnp.pad(counts, ((0, 0), (0, 0), (0, lanes - rounds * station_count)))
    ext = jnp.concatenate([cross, counts], axis=1)

    wins = lax.axis_size("win")
    if wins == 2 and bands == 2:
        per_band = station_count // (wins * bands)
        me = lax.axis_index("win") * bands + band_index
        pieces = []
        for flip in range(wins * bands):
            chunk = lax.dynamic_slice_in_dim(ext, (me ^ flip) * per_band, per_band, 0)
            if flip:
                perm = [(k, k ^ flip) for k in range(wins * bands)]
                chunk = lax.ppermute(chunk, ("win", "band"), perm)
            pieces.append(chunk)
        same = pieces[0] + pieces[2]
        other = pieces[1] + pieces[3]
        first = jnp.where(band_index == 0, same, other)
        second = jnp.where(band_index == 0, other, same)
        swapped = jnp.stack([first, second], axis=0)
        totals = same[:, per_station, : rounds * station_count]
    else:
        summed = lax.psum_scatter(ext, "win", scatter_dimension=0, tiled=True)
        per_band = summed.shape[0] // bands
        summed = summed.reshape((bands, per_band) + summed.shape[1:])
        swapped = lax.all_to_all(summed, "band", split_axis=0, concat_axis=0, tiled=True)
        totals = swapped[0, :, per_station, : rounds * station_count]
    totals = totals.reshape(per_band, 1, rounds, 1, station_count, 1)
    spec = swapped[:bands, :, :per_station, :].transpose(1, 2, 0, 3)
    spec = spec.reshape(per_band, comp_count, rounds, comp_count, station_count, bands * lanes)
    stacked = spec / jnp.maximum(totals, 1.0)

    full_lag = lag_table(sample_points, FREQ, 0, NLAG, FREQ)
    full_lag = full_lag.reshape(2, bands, nb, NLAG).transpose(1, 0, 2, 3).reshape(-1, NLAG)
    lagged = jnp.einsum(
        "iarbje,el->riabjl",
        stacked,
        full_lag,
        precision=lax.Precision.HIGHEST,
        preferred_element_type=jnp.float32,
    )
    return lagged.reshape(rounds, per_band, comp_count, comp_count * station_count, NLAG)


def solution(mesh):
    placed = (P(("hours", "win"), None, "pair", None), P(("hours", "win"), "pair"), P())
    return jax.shard_map(
        body,
        mesh=mesh,
        in_specs=placed,
        out_specs=P(None, ("hours", "pair", "win", "band"), None, None, None),
        check_vma=False,
    )
```

```python
import math

import jax
import jax.numpy as jnp
from jax import lax
from jax.experimental import pallas as pl
from jax.experimental.pallas import tpu as pltpu
from jax.sharding import PartitionSpec as P

FREQ = 128
NLAG = 256
ROUNDS = 4
WSTEP = 4


def dft_table(sample_points, bin_count, first_bin):
    sample_moments = jnp.arange(sample_points, dtype=jnp.int32)
    spectral_bin_index = first_bin + 1 + jnp.arange(bin_count, dtype=jnp.int32)
    phase_turns = jnp.mod(sample_moments[:, None] * spectral_bin_index[None, :], sample_points)
    phases = phase_turns.astype(jnp.float32) * (2.0 * math.pi / sample_points)
    hanning_taper = 0.5 - 0.5 * jnp.cos(
        sample_moments.astype(jnp.float32) * (2.0 * math.pi / sample_points)
    )
    weight = (hanning_taper * math.sqrt(8.0 / (3.0 * sample_points)))[:, None]
    return jnp.concatenate([weight * jnp.cos(phases), -(weight * jnp.sin(phases))], axis=1).astype(
        jnp.bfloat16
    )


def lag_table(sample_points, bin_count, first_bin, lag_count, all_bins):
    spectral_bin_index = first_bin + 1 + jnp.arange(bin_count, dtype=jnp.int32)
    shifts = jnp.arange(lag_count, dtype=jnp.int32) - lag_count // 2
    phase_turns = jnp.mod(spectral_bin_index[:, None] * shifts[None, :], sample_points)
    phases = phase_turns.astype(jnp.float32) * (2.0 * math.pi / sample_points)
    lag_scale = 1.0 / math.sqrt(all_bins)
    return jnp.concatenate([jnp.cos(phases) * lag_scale, -(jnp.sin(phases) * lag_scale)], axis=0)


def whiten(spectra, validity):
    bin_count = spectra.shape[-1] // 2
    real_part = spectra[..., :bin_count]
    imag_part = spectra[..., bin_count:]
    band_power = jnp.mean(real_part * real_part + imag_part * imag_part, axis=1)
    amplitude = jnp.sqrt(jnp.maximum(band_power, 0.25))
    factor = validity[:, :, None] / amplitude
    factor = jnp.concatenate([factor, factor], axis=-1)
    return (spectra * factor[:, None]).astype(jnp.bfloat16)


def cross_kernel(own_ref, part_ref, out_ref):
    window_count, comp_count, station_count, lanes = own_ref.shape
    nb = lanes // 2
    rows = lax.broadcasted_iota(jnp.int32, (station_count, lanes), 0)
    lower = lax.broadcasted_iota(jnp.int32, (station_count, lanes), 1) < nb
    moved = [pltpu.roll(rows, k, 0) if k else rows for k in range(station_count)]
    zero = tuple(jnp.zeros((station_count, lanes), jnp.float32) for _ in range(station_count))
    for a in range(comp_count):
        for b in range(part_ref.shape[2]):

            def step(k, carry):
                direct, turned = list(carry[0]), list(carry[1])
                for u in range(WSTEP):
                    w = k * WSTEP + u
                    a_tile = own_ref[w, a]
                    b_tile = part_ref[0, w, b]
                    b_turn = pltpu.roll(b_tile, nb, 1)
                    for d in range(station_count):
                        a_rot = pltpu.roll(a_tile, d, 0) if d else a_tile
                        direct[d] = direct[d] + a_rot * b_tile
                        turned[d] = turned[d] + a_rot * b_turn
                return tuple(direct), tuple(turned)

            direct, turned = lax.fori_loop(0, window_count // WSTEP, step, (zero, zero))
            for i in range(station_count):
                dsum = jnp.where(moved[0] == i, direct[0], 0.0)
                tsum = jnp.where(moved[0] == i, turned[0], 0.0)
                for d in range(1, station_count):
                    dsum = jnp.where(moved[d] == i, direct[d], dsum)
                    tsum = jnp.where(moved[d] == i, turned[d], tsum)
                real = dsum + pltpu.roll(dsum, nb, 1)
                imag = tsum - pltpu.roll(tsum, nb, 1)
                out_ref[i, a, 0, b] = jnp.where(lower, real, imag)


def cross_products(own, partners):
    rounds, window_count, comp_count, station_count, lanes = partners.shape
    flops = 4 * rounds * window_count * comp_count * comp_count * station_count * station_count * lanes
    return pl.pallas_call(
        cross_kernel,
        grid=(rounds,),
        in_specs=[
            pl.BlockSpec((window_count, comp_count, station_count, lanes), lambda r: (0, 0, 0, 0)),
            pl.BlockSpec(
                (1, window_count, comp_count, station_count, lanes), lambda r: (r, 0, 0, 0, 0)
            ),
        ],
        out_specs=pl.BlockSpec(
            (station_count, comp_count, 1, comp_count, station_count, lanes),
            lambda r: (0, 0, r, 0, 0, 0),
        ),
        out_shape=jax.ShapeDtypeStruct(
            (station_count, comp_count, rounds, comp_count, station_count, lanes), jnp.float32
        ),
        cost_estimate=pl.CostEstimate(
            flops=flops,
            transcendentals=0,
            bytes_accessed=4 * (own.size + partners.size + station_count * comp_count * rounds * comp_count * station_count * lanes),
        ),
    )(own, partners)


def body(records, valid_mask, round_keys):
    window_count, comp_count, station_count, sample_points = records.shape
    bands = lax.axis_size("band")
    band_index = lax.axis_index("band")
    pair_index = lax.axis_index("pair")
    nb = FREQ // bands
    lanes = 2 * nb
    rounds = round_keys.shape[0]
    rows = window_count * comp_count * station_count

    dft_rows = dft_table(sample_points, nb, band_index * nb)
    spectra = jnp.einsum("wcsn,nk->wcsk", records, dft_rows, preferred_element_type=jnp.float32)
    validity = valid_mask.astype(jnp.float32)
    whitened = whiten(spectra, validity)

    vrows = -(-window_count * station_count // lanes)
    vflat = validity.astype(jnp.bfloat16).reshape(-1)
    vflat = jnp.pad(vflat, (0, vrows * lanes - vflat.shape[0])).reshape(vrows, lanes)
    payload = jnp.concatenate([whitened.reshape(rows, lanes), vflat], axis=0)

    gathered = lax.all_gather(payload, "pair", axis=0, tiled=False)
    partner_list = jnp.bitwise_xor(pair_index, round_keys)
    partners = jnp.take(gathered, partner_list, axis=0, mode="clip")
    partner_valid = partners[:, rows:].reshape(rounds, -1)[:, : window_count * station_count]
    partner_valid = partner_valid.reshape(rounds, window_count, station_count).astype(jnp.float32)
    partner_spec = partners[:, :rows].astype(jnp.float32).reshape(
        rounds, window_count, comp_count, station_count, lanes
    )

    cross = cross_products(whitened.astype(jnp.float32), partner_spec)
    per_station = comp_count * rounds * comp_count * station_count
    cross = cross.reshape(station_count, per_station, lanes)

    counts = jnp.einsum("wi,rwj->irj", validity, partner_valid)
    counts = counts.reshape(station_count, 1, rounds * station_count)
    counts = jnp.pad(counts, ((0, 0), (0, 0), (0, lanes - rounds * station_count)))
    ext = jnp.concatenate([cross, counts], axis=1)

    wins = lax.axis_size("win")
    if wins == 2 and bands == 2:
        per_band = station_count // (wins * bands)
        me = lax.axis_index("win") * bands + band_index
        pieces = []
        for flip in range(wins * bands):
            chunk = lax.dynamic_slice_in_dim(ext, (me ^ flip) * per_band, per_band, 0)
            if flip:
                perm = [(k, k ^ flip) for k in range(wins * bands)]
                chunk = lax.ppermute(chunk, ("win", "band"), perm)
            pieces.append(chunk)
        same = pieces[0] + pieces[2]
        other = pieces[1] + pieces[3]
        first = jnp.where(band_index == 0, same, other)
        second = jnp.where(band_index == 0, other, same)
        swapped = jnp.stack([first, second], axis=0)
        totals = same[:, per_station, : rounds * station_count]
    else:
        summed = lax.psum_scatter(ext, "win", scatter_dimension=0, tiled=True)
        per_band = summed.shape[0] // bands
        summed = summed.reshape((bands, per_band) + summed.shape[1:])
        swapped = lax.all_to_all(summed, "band", split_axis=0, concat_axis=0, tiled=True)
        totals = swapped[0, :, per_station, : rounds * station_count]
    totals = totals.reshape(per_band, 1, rounds, 1, station_count, 1)
    spec = swapped[:bands, :, :per_station, :].transpose(1, 2, 0, 3)
    spec = spec.reshape(per_band, comp_count, rounds, comp_count, station_count, bands * lanes)
    stacked = spec / jnp.maximum(totals, 1.0)

    full_lag = lag_table(sample_points, FREQ, 0, NLAG, FREQ)
    full_lag = full_lag.reshape(2, bands, nb, NLAG).transpose(1, 0, 2, 3).reshape(-1, NLAG)
    lagged = jnp.einsum(
        "iarbje,el->riabjl",
        stacked,
        full_lag,
        precision=lax.Precision.HIGHEST,
        preferred_element_type=jnp.float32,
    )
    return lagged.reshape(rounds, per_band, comp_count, comp_count * station_count, NLAG)


def solution(mesh):
    placed = (P(("hours", "win"), None, "pair", None), P(("hours", "win"), "pair"), P())
    return jax.shard_map(
        body,
        mesh=mesh,
        in_specs=placed,
        out_specs=P(None, ("hours", "pair", "win", "band"), None, None, None),
        check_vma=False,
    )
```

```python
import math

import jax
import jax.numpy as jnp
from jax import lax
from jax.experimental import pallas as pl
from jax.experimental.pallas import tpu as pltpu
from jax.sharding import PartitionSpec as P

FREQ = 128
NLAG = 256
ROUNDS = 4
WSTEP = 4


def dft_table(sample_points, bin_count, first_bin):
    sample_moments = jnp.arange(sample_points, dtype=jnp.int32)
    spectral_bin_index = first_bin + 1 + jnp.arange(bin_count, dtype=jnp.int32)
    phase_turns = jnp.mod(sample_moments[:, None] * spectral_bin_index[None, :], sample_points)
    phases = phase_turns.astype(jnp.float32) * (2.0 * math.pi / sample_points)
    hanning_taper = 0.5 - 0.5 * jnp.cos(
        sample_moments.astype(jnp.float32) * (2.0 * math.pi / sample_points)
    )
    weight = (hanning_taper * math.sqrt(8.0 / (3.0 * sample_points)))[:, None]
    return jnp.concatenate([weight * jnp.cos(phases), -(weight * jnp.sin(phases))], axis=1).astype(
        jnp.bfloat16
    )


def lag_table(sample_points, bin_count, first_bin, lag_count, all_bins):
    spectral_bin_index = first_bin + 1 + jnp.arange(bin_count, dtype=jnp.int32)
    shifts = jnp.arange(lag_count, dtype=jnp.int32) - lag_count // 2
    phase_turns = jnp.mod(spectral_bin_index[:, None] * shifts[None, :], sample_points)
    phases = phase_turns.astype(jnp.float32) * (2.0 * math.pi / sample_points)
    lag_scale = 1.0 / math.sqrt(all_bins)
    return jnp.concatenate([jnp.cos(phases) * lag_scale, -(jnp.sin(phases) * lag_scale)], axis=0)


def whiten(spectra, validity):
    bin_count = spectra.shape[-1] // 2
    real_part = spectra[..., :bin_count]
    imag_part = spectra[..., bin_count:]
    band_power = jnp.mean(real_part * real_part + imag_part * imag_part, axis=1)
    amplitude = jnp.sqrt(jnp.maximum(band_power, 0.25))
    factor = validity[:, :, None] / amplitude
    factor = jnp.concatenate([factor, factor], axis=-1)
    return (spectra * factor[:, None]).astype(jnp.bfloat16)


def dft_kernel(rec_ref, table_ref, valid_ref, out_ref):
    station_count, window_count = valid_ref.shape
    comp_count = rec_ref.shape[0] // station_count
    nb = table_ref.shape[0] // 2
    table = table_ref[...]
    for s in range(station_count):
        parts = []
        for c in range(comp_count):
            z = lax.dot_general(
                table,
                rec_ref[c * station_count + s],
                (((1,), (1,)), ((), ())),
                preferred_element_type=jnp.float32,
            )
            parts.append((z[:nb], z[nb:]))
        total = parts[0][0] * parts[0][0] + parts[0][1] * parts[0][1]
        for c in range(1, comp_count):
            total = total + (parts[c][0] * parts[c][0] + parts[c][1] * parts[c][1])
        band_power = total / float(comp_count)
        amplitude = jnp.sqrt(jnp.maximum(band_power, 0.25))
        factor = valid_ref[pl.ds(s, 1), :] / amplitude
        for c in range(comp_count):
            out_ref[c * station_count + s, :, pl.ds(0, window_count)] = parts[c][0] * factor
            out_ref[c * station_count + s, :, pl.ds(window_count, window_count)] = parts[c][1] * factor


def dft_whiten(rec_t, table_t, valid_t):
    rows, window_count, sample_points = rec_t.shape
    nb = table_t.shape[0] // 2
    return pl.pallas_call(
        dft_kernel,
        out_shape=jax.ShapeDtypeStruct((rows, nb, 2 * window_count), jnp.float32),
        cost_estimate=pl.CostEstimate(
            flops=2 * rows * window_count * sample_points * 2 * nb,
            transcendentals=rows * nb * window_count,
            bytes_accessed=2 * rec_t.size + 2 * table_t.size + 4 * rows * nb * 2 * window_count,
        ),
    )(rec_t, table_t, valid_t)


def body(records, valid_mask, round_keys):
    window_count, comp_count, station_count, sample_points = records.shape
    bands = lax.axis_size("band")
    wins = lax.axis_size("win")
    band_index = lax.axis_index("band")
    pair_index = lax.axis_index("pair")
    nb = FREQ // bands
    lanes = 2 * window_count
    rounds = round_keys.shape[0]
    xs = comp_count * station_count

    dft_rows = dft_table(sample_points, nb, band_index * nb)
    rec_t = records.reshape(window_count, xs, sample_points).transpose(1, 0, 2)
    validity = valid_mask.astype(jnp.float32)
    spec = dft_whiten(rec_t, dft_rows.T, validity.T).astype(jnp.bfloat16)

    vrows = -(-window_count * station_count // lanes)
    vflat = validity.astype(jnp.bfloat16).reshape(-1)
    vflat = jnp.pad(vflat, (0, vrows * lanes - vflat.shape[0])).reshape(vrows, lanes)
    payload = jnp.concatenate([spec.reshape(xs * nb, lanes), vflat], axis=0)

    gathered = lax.all_gather(payload, "pair", axis=0, tiled=False)
    partner_list = jnp.bitwise_xor(pair_index, round_keys)
    partners = jnp.take(gathered, partner_list, axis=0, mode="clip")
    partner_valid = partners[:, xs * nb :].reshape(rounds, -1)[:, : window_count * station_count]
    partner_valid = partner_valid.reshape(rounds, window_count, station_count).astype(jnp.float32)
    other = partners[:, : xs * nb].reshape(rounds, xs, nb, lanes)

    half = lax.broadcasted_iota(jnp.int32, (lanes,), 0) < window_count
    turned = jnp.roll(other, window_count, axis=-1) * jnp.where(half, -1.0, 1.0).astype(jnp.bfloat16)
    rhs = jnp.stack([other, turned], axis=0)
    rhs = rhs.transpose(3, 0, 1, 2, 4).reshape(nb, 2 * rounds * xs, lanes)
    lhs = spec.transpose(1, 0, 2)
    prod = jnp.einsum("fxk,fyk->fxy", lhs, rhs, preferred_element_type=jnp.float32)
    prod = prod.reshape(nb, comp_count, station_count, 2 * rounds * xs)

    counts = jnp.einsum("wi,rwj->irj", validity, partner_valid).reshape(station_count, rounds * station_count)
    slab = jnp.zeros((1, comp_count, station_count, 2 * rounds * xs), jnp.float32)
    slab = slab.at[0, 0, :, : rounds * station_count].set(counts)
    ext = jnp.concatenate([prod, slab], axis=0)

    group = wins * bands
    per_dev = station_count // group
    me = lax.axis_index("win") * bands + band_index
    by_offset = [None] * bands
    for shift in range(group):
        dest = (me + shift) % group
        chunk = lax.dynamic_slice_in_dim(ext, dest * per_dev, per_dev, 2)
        if shift:
            perm = [(k, (k + shift) % group) for k in range(group)]
            chunk = lax.ppermute(chunk, ("win", "band"), perm)
        q = shift % bands
        by_offset[q] = chunk if by_offset[q] is None else by_offset[q] + chunk
    totals = by_offset[0][nb, 0, :, : rounds * station_count].reshape(per_dev, rounds, station_count)
    ordered = []
    for bb in range(bands):
        pick = by_offset[0]
        for q in range(1, bands):
            pick = jnp.where((band_index - q) % bands == bb, by_offset[q], pick)
        ordered.append(pick[:nb])
    stacked = jnp.stack(ordered, axis=0)
    stacked = stacked.reshape(bands, nb, comp_count, per_dev, 2, rounds, comp_count, station_count)
    divisor = jnp.maximum(totals, 1.0)[None, None, None, :, None, :, None, :]
    stacked = stacked / divisor

    full_lag = lag_table(sample_points, FREQ, 0, NLAG, FREQ)
    full_lag = full_lag.reshape(2, bands, nb, NLAG).transpose(1, 0, 2, 3)
    lagged = jnp.einsum(
        "gfaiurbj,gufl->riabjl",
        stacked,
        full_lag,
        precision=lax.Precision.HIGHEST,
        preferred_element_type=jnp.float32,
    )
    return lagged.reshape(rounds, per_dev, comp_count, comp_count * station_count, NLAG)


def solution(mesh):
    placed = (P(("hours", "win"), None, "pair", None), P(("hours", "win"), "pair"), P())
    return jax.shard_map(
        body,
        mesh=mesh,
        in_specs=placed,
        out_specs=P(None, ("hours", "pair", "win", "band"), None, None, None),
        check_vma=False,
    )
```

```python
import math

import jax
import jax.numpy as jnp
from jax import lax
from jax.experimental import pallas as pl
from jax.experimental.pallas import tpu as pltpu
from jax.sharding import PartitionSpec as P

FREQ = 128
NLAG = 256
ROUNDS = 4
WSTEP = 4


def dft_table(sample_points, bin_count, first_bin):
    sample_moments = jnp.arange(sample_points, dtype=jnp.int32)
    spectral_bin_index = first_bin + 1 + jnp.arange(bin_count, dtype=jnp.int32)
    phase_turns = jnp.mod(sample_moments[:, None] * spectral_bin_index[None, :], sample_points)
    phases = phase_turns.astype(jnp.float32) * (2.0 * math.pi / sample_points)
    hanning_taper = 0.5 - 0.5 * jnp.cos(
        sample_moments.astype(jnp.float32) * (2.0 * math.pi / sample_points)
    )
    weight = (hanning_taper * math.sqrt(8.0 / (3.0 * sample_points)))[:, None]
    return jnp.concatenate([weight * jnp.cos(phases), -(weight * jnp.sin(phases))], axis=1).astype(
        jnp.bfloat16
    )


def lag_table(sample_points, bin_count, first_bin, lag_count, all_bins):
    spectral_bin_index = first_bin + 1 + jnp.arange(bin_count, dtype=jnp.int32)
    shifts = jnp.arange(lag_count, dtype=jnp.int32) - lag_count // 2
    phase_turns = jnp.mod(spectral_bin_index[:, None] * shifts[None, :], sample_points)
    phases = phase_turns.astype(jnp.float32) * (2.0 * math.pi / sample_points)
    lag_scale = 1.0 / math.sqrt(all_bins)
    return jnp.concatenate([jnp.cos(phases) * lag_scale, -(jnp.sin(phases) * lag_scale)], axis=0)


def whiten(spectra, validity):
    bin_count = spectra.shape[-1] // 2
    real_part = spectra[..., :bin_count]
    imag_part = spectra[..., bin_count:]
    band_power = jnp.mean(real_part * real_part + imag_part * imag_part, axis=1)
    amplitude = jnp.sqrt(jnp.maximum(band_power, 0.25))
    factor = validity[:, :, None] / amplitude
    factor = jnp.concatenate([factor, factor], axis=-1)
    return (spectra * factor[:, None]).astype(jnp.bfloat16)


def dft_kernel(rec_ref, table_ref, valid_ref, out_ref):
    station_count, window_count = valid_ref.shape
    comp_count = rec_ref.shape[0] // station_count
    nb = table_ref.shape[0] // 2
    table = table_ref[...]
    zero_row = jnp.zeros((1, window_count), jnp.float32)
    for s in range(station_count):
        parts = []
        for c in range(comp_count):
            z = lax.dot_general(
                table,
                rec_ref[c * station_count + s],
                (((1,), (1,)), ((), ())),
                preferred_element_type=jnp.float32,
            )
            parts.append((z[:nb], z[nb:]))
        total = parts[0][0] * parts[0][0] + parts[0][1] * parts[0][1]
        for c in range(1, comp_count):
            total = total + (parts[c][0] * parts[c][0] + parts[c][1] * parts[c][1])
        band_power = total / float(comp_count)
        amplitude = jnp.sqrt(jnp.maximum(band_power, 0.25))
        valid_row = valid_ref[pl.ds(s, 1), :]
        factor = valid_row / amplitude
        for c in range(comp_count):
            x = c * station_count + s
            out_ref[x, pl.ds(0, 1), pl.ds(0, window_count)] = valid_row if c == 0 else zero_row
            out_ref[x, pl.ds(0, 1), pl.ds(window_count, window_count)] = zero_row
            out_ref[x, pl.ds(1, nb), pl.ds(0, window_count)] = parts[c][0] * factor
            out_ref[x, pl.ds(1, nb), pl.ds(window_count, window_count)] = parts[c][1] * factor


def dft_whiten(rec_t, table_t, valid_t):
    rows, window_count, sample_points = rec_t.shape
    nb = table_t.shape[0] // 2
    return pl.pallas_call(
        dft_kernel,
        out_shape=jax.ShapeDtypeStruct((rows, 1 + nb, 2 * window_count), jnp.float32),
        cost_estimate=pl.CostEstimate(
            flops=2 * rows * window_count * sample_points * 2 * nb,
            transcendentals=rows * nb * window_count,
            bytes_accessed=2 * rec_t.size + 2 * table_t.size + 4 * rows * (nb + 1) * 2 * window_count,
        ),
    )(rec_t, table_t, valid_t)


def exchange(prod, station_count, bands, band_index):
    group = lax.axis_size("win") * bands
    per_dev = station_count // group
    me = lax.axis_index("win") * bands + band_index
    by_offset = [None] * bands
    for shift in range(group):
        dest = (me + shift) % group
        chunk = lax.dynamic_slice_in_dim(prod, dest * per_dev, per_dev, 2)
        if shift:
            perm = [(k, (k + shift) % group) for k in range(group)]
            chunk = lax.ppermute(chunk, ("win", "band"), perm)
        q = shift % bands
        by_offset[q] = chunk if by_offset[q] is None else by_offset[q] + chunk
    ordered = []
    for bb in range(bands):
        pick = by_offset[0]
        for q in range(1, bands):
            pick = jnp.where((band_index - q) % bands == bb, by_offset[q], pick)
        ordered.append(pick)
    return jnp.stack(ordered, axis=0), by_offset[0]


def body(records, valid_mask, round_keys):
    window_count, comp_count, station_count, sample_points = records.shape
    bands = lax.axis_size("band")
    band_index = lax.axis_index("band")
    pair_index = lax.axis_index("pair")
    nb = FREQ // bands
    rounds = round_keys.shape[0]
    xs = comp_count * station_count
    lanes = 2 * window_count
    slots = nb + 1

    dft_rows = dft_table(sample_points, nb, band_index * nb)
    rec_t = records.reshape(window_count, xs, sample_points).transpose(1, 0, 2)
    validity = valid_mask.astype(jnp.float32)
    spec = dft_whiten(rec_t, dft_rows.T, validity.T).astype(jnp.bfloat16)

    gathered = lax.all_gather(spec.reshape(xs * slots, lanes), "pair", axis=0, tiled=False)
    partner_list = jnp.bitwise_xor(pair_index, round_keys)
    other = jnp.take(gathered, partner_list, axis=0, mode="clip").reshape(rounds, xs, slots, lanes)
    rhs = other.transpose(2, 0, 1, 3).reshape(slots, rounds * xs, lanes)

    half = lax.broadcasted_iota(jnp.int32, (lanes,), 0) < window_count
    turned = jnp.roll(spec, window_count, axis=-1) * jnp.where(half, 1.0, -1.0).astype(jnp.bfloat16)
    lhs = jnp.stack([spec, turned], axis=0).transpose(2, 0, 1, 3).reshape(slots, 2 * xs, lanes)
    prod = jnp.einsum("fxk,fyk->fxy", lhs, rhs, preferred_element_type=jnp.float32)
    prod = prod.reshape(slots, 2 * comp_count, station_count, rounds * xs)

    stacked, same = exchange(prod, station_count, bands, band_index)
    per_dev = stacked.shape[3]
    totals = same[0, 0].reshape(per_dev, rounds, comp_count, station_count)[:, :, 0, :]
    stacked = stacked[:, 1:].reshape(
        bands, nb, 2, comp_count, per_dev, rounds, comp_count, station_count
    )

    full_lag = lag_table(sample_points, FREQ, 0, NLAG, FREQ)
    full_lag = full_lag.reshape(2, bands, nb, NLAG).transpose(1, 0, 2, 3)
    lagged = jnp.einsum(
        "gfuairbj,gufl->riabjl",
        stacked,
        full_lag,
        precision=lax.Precision.HIGHEST,
        preferred_element_type=jnp.float32,
    )
    divisor = jnp.maximum(totals, 1.0).transpose(1, 0, 2)[:, :, None, None, :, None]
    lagged = lagged / divisor
    return lagged.reshape(rounds, per_dev, comp_count, comp_count * station_count, NLAG)


def solution(mesh):
    placed = (P(("hours", "win"), None, "pair", None), P(("hours", "win"), "pair"), P())
    return jax.shard_map(
        body,
        mesh=mesh,
        in_specs=placed,
        out_specs=P(None, ("hours", "pair", "win", "band"), None, None, None),
        check_vma=False,
    )
```

```python
import math

import jax
import jax.numpy as jnp
from jax import lax
from jax.experimental import pallas as pl
from jax.experimental.pallas import tpu as pltpu
from jax.sharding import PartitionSpec as P

FREQ = 128
NLAG = 256
ROUNDS = 4
WSTEP = 4


def dft_table(sample_points, bin_count, first_bin):
    sample_moments = jnp.arange(sample_points, dtype=jnp.int32)
    spectral_bin_index = first_bin + 1 + jnp.arange(bin_count, dtype=jnp.int32)
    phase_turns = jnp.mod(sample_moments[:, None] * spectral_bin_index[None, :], sample_points)
    phases = phase_turns.astype(jnp.float32) * (2.0 * math.pi / sample_points)
    hanning_taper = 0.5 - 0.5 * jnp.cos(
        sample_moments.astype(jnp.float32) * (2.0 * math.pi / sample_points)
    )
    weight = (hanning_taper * math.sqrt(8.0 / (3.0 * sample_points)))[:, None]
    return jnp.concatenate([weight * jnp.cos(phases), -(weight * jnp.sin(phases))], axis=1).astype(
        jnp.bfloat16
    )


def lag_table(sample_points, bin_count, first_bin, lag_count, all_bins):
    spectral_bin_index = first_bin + 1 + jnp.arange(bin_count, dtype=jnp.int32)
    shifts = jnp.arange(lag_count, dtype=jnp.int32) - lag_count // 2
    phase_turns = jnp.mod(spectral_bin_index[:, None] * shifts[None, :], sample_points)
    phases = phase_turns.astype(jnp.float32) * (2.0 * math.pi / sample_points)
    lag_scale = 1.0 / math.sqrt(all_bins)
    return jnp.concatenate([jnp.cos(phases) * lag_scale, -(jnp.sin(phases) * lag_scale)], axis=0)


def whiten(spectra, validity):
    bin_count = spectra.shape[-1] // 2
    real_part = spectra[..., :bin_count]
    imag_part = spectra[..., bin_count:]
    band_power = jnp.mean(real_part * real_part + imag_part * imag_part, axis=1)
    amplitude = jnp.sqrt(jnp.maximum(band_power, 0.25))
    factor = validity[:, :, None] / amplitude
    factor = jnp.concatenate([factor, factor], axis=-1)
    return (spectra * factor[:, None]).astype(jnp.bfloat16)


def dft_kernel(rec_ref, table_ref, valid_ref, out_ref):
    station_count, window_count = valid_ref.shape
    comp_count = rec_ref.shape[0] // station_count
    nb = table_ref.shape[0] // 2
    table = table_ref[...]
    zero_row = jnp.zeros((1, window_count), jnp.float32)
    for s in range(station_count):
        parts = []
        for c in range(comp_count):
            z = lax.dot_general(
                table,
                rec_ref[c * station_count + s],
                (((1,), (1,)), ((), ())),
                preferred_element_type=jnp.float32,
            )
            parts.append((z[:nb], z[nb:]))
        total = parts[0][0] * parts[0][0] + parts[0][1] * parts[0][1]
        for c in range(1, comp_count):
            total = total + (parts[c][0] * parts[c][0] + parts[c][1] * parts[c][1])
        band_power = total / float(comp_count)
        amplitude = jnp.sqrt(jnp.maximum(band_power, 0.25))
        valid_row = valid_ref[pl.ds(s, 1), :]
        factor = valid_row / amplitude
        for c in range(comp_count):
            x = c * station_count + s
            out_ref[x, pl.ds(0, 1), pl.ds(0, window_count)] = valid_row if c == 0 else zero_row
            out_ref[x, pl.ds(0, 1), pl.ds(window_count, window_count)] = zero_row
            out_ref[x, pl.ds(1, nb), pl.ds(0, window_count)] = parts[c][0] * factor
            out_ref[x, pl.ds(1, nb), pl.ds(window_count, window_count)] = parts[c][1] * factor


def dft_whiten(rec_t, table_t, valid_t):
    rows, window_count, sample_points = rec_t.shape
    nb = table_t.shape[0] // 2
    return pl.pallas_call(
        dft_kernel,
        out_shape=jax.ShapeDtypeStruct((rows, 1 + nb, 2 * window_count), jnp.float32),
        cost_estimate=pl.CostEstimate(
            flops=2 * rows * window_count * sample_points * 2 * nb,
            transcendentals=rows * nb * window_count,
            bytes_accessed=2 * rec_t.size + 2 * table_t.size + 4 * rows * (nb + 1) * 2 * window_count,
        ),
    )(rec_t, table_t, valid_t)


def exchange(prod, station_count, bands, band_index):
    group = lax.axis_size("win") * bands
    per_dev = station_count // group
    me = lax.axis_index("win") * bands + band_index
    by_offset = [None] * bands
    for shift in range(group):
        dest = (me + shift) % group
        chunk = lax.dynamic_slice_in_dim(prod, dest * per_dev, per_dev, 2)
        if shift:
            perm = [(k, (k + shift) % group) for k in range(group)]
            chunk = lax.ppermute(chunk.astype(jnp.bfloat16), ("win", "band"), perm)
            chunk = chunk.astype(jnp.float32)
        q = shift % bands
        by_offset[q] = chunk if by_offset[q] is None else by_offset[q] + chunk
    ordered = []
    for bb in range(bands):
        pick = by_offset[0]
        for q in range(1, bands):
            pick = jnp.where((band_index - q) % bands == bb, by_offset[q], pick)
        ordered.append(pick)
    return jnp.stack(ordered, axis=0), by_offset[0]


def body(records, valid_mask, round_keys):
    window_count, comp_count, station_count, sample_points = records.shape
    bands = lax.axis_size("band")
    band_index = lax.axis_index("band")
    pair_index = lax.axis_index("pair")
    nb = FREQ // bands
    rounds = round_keys.shape[0]
    xs = comp_count * station_count
    lanes = 2 * window_count
    slots = nb + 1

    dft_rows = dft_table(sample_points, nb, band_index * nb)
    rec_t = records.reshape(window_count, xs, sample_points).transpose(1, 0, 2)
    validity = valid_mask.astype(jnp.float32)
    spec = dft_whiten(rec_t, dft_rows.T, validity.T).astype(jnp.bfloat16)

    gathered = lax.all_gather(spec.reshape(xs * slots, lanes), "pair", axis=0, tiled=False)
    partner_list = jnp.bitwise_xor(pair_index, round_keys)
    other = jnp.take(gathered, partner_list, axis=0, mode="clip").reshape(rounds, xs, slots, lanes)
    rhs = other.transpose(2, 0, 1, 3).reshape(slots, rounds * xs, lanes)

    half = lax.broadcasted_iota(jnp.int32, (lanes,), 0) < window_count
    turned = jnp.roll(spec, window_count, axis=-1) * jnp.where(half, 1.0, -1.0).astype(jnp.bfloat16)
    lhs = jnp.stack([spec, turned], axis=0).transpose(2, 0, 1, 3).reshape(slots, 2 * xs, lanes)
    prod = jnp.einsum("fxk,fyk->fxy", lhs, rhs, preferred_element_type=jnp.float32)
    prod = prod.reshape(slots, 2 * comp_count, station_count, rounds * xs)

    stacked, same = exchange(prod, station_count, bands, band_index)
    per_dev = stacked.shape[3]
    totals = same[0, 0].reshape(per_dev, rounds, comp_count, station_count)[:, :, 0, :]
    stacked = stacked[:, 1:].reshape(
        bands, nb, 2, comp_count, per_dev, rounds, comp_count, station_count
    )

    full_lag = lag_table(sample_points, FREQ, 0, NLAG, FREQ)
    full_lag = full_lag.reshape(2, bands, nb, NLAG).transpose(1, 0, 2, 3)
    lagged = jnp.einsum(
        "gfuairbj,gufl->riabjl",
        stacked,
        full_lag,
        precision=lax.Precision.HIGHEST,
        preferred_element_type=jnp.float32,
    )
    divisor = jnp.maximum(totals, 1.0).transpose(1, 0, 2)[:, :, None, None, :, None]
    lagged = lagged / divisor
    return lagged.reshape(rounds, per_dev, comp_count, comp_count * station_count, NLAG)


def solution(mesh):
    placed = (P(("hours", "win"), None, "pair", None), P(("hours", "win"), "pair"), P())
    return jax.shard_map(
        body,
        mesh=mesh,
        in_specs=placed,
        out_specs=P(None, ("hours", "pair", "win", "band"), None, None, None),
        check_vma=False,
    )
```

```python
import math

import jax
import jax.numpy as jnp
from jax import lax
from jax.experimental import pallas as pl
from jax.experimental.pallas import tpu as pltpu
from jax.sharding import PartitionSpec as P

FREQ = 128
NLAG = 256
ROUNDS = 4
WSTEP = 4


def dft_table(sample_points, bin_count, first_bin):
    sample_moments = jnp.arange(sample_points, dtype=jnp.int32)
    spectral_bin_index = first_bin + 1 + jnp.arange(bin_count, dtype=jnp.int32)
    phase_turns = jnp.mod(sample_moments[:, None] * spectral_bin_index[None, :], sample_points)
    phases = phase_turns.astype(jnp.float32) * (2.0 * math.pi / sample_points)
    hanning_taper = 0.5 - 0.5 * jnp.cos(
        sample_moments.astype(jnp.float32) * (2.0 * math.pi / sample_points)
    )
    weight = (hanning_taper * math.sqrt(8.0 / (3.0 * sample_points)))[:, None]
    return jnp.concatenate([weight * jnp.cos(phases), -(weight * jnp.sin(phases))], axis=1).astype(
        jnp.bfloat16
    )


def lag_table(sample_points, bin_count, first_bin, lag_count, all_bins):
    spectral_bin_index = first_bin + 1 + jnp.arange(bin_count, dtype=jnp.int32)
    shifts = jnp.arange(lag_count, dtype=jnp.int32) - lag_count // 2
    phase_turns = jnp.mod(spectral_bin_index[:, None] * shifts[None, :], sample_points)
    phases = phase_turns.astype(jnp.float32) * (2.0 * math.pi / sample_points)
    lag_scale = 1.0 / math.sqrt(all_bins)
    return jnp.concatenate([jnp.cos(phases) * lag_scale, -(jnp.sin(phases) * lag_scale)], axis=0)


def whiten(spectra, validity):
    bin_count = spectra.shape[-1] // 2
    real_part = spectra[..., :bin_count]
    imag_part = spectra[..., bin_count:]
    band_power = jnp.mean(real_part * real_part + imag_part * imag_part, axis=1)
    amplitude = jnp.sqrt(jnp.maximum(band_power, 0.25))
    factor = validity[:, :, None] / amplitude
    factor = jnp.concatenate([factor, factor], axis=-1)
    return (spectra * factor[:, None]).astype(jnp.bfloat16)


def dft_kernel(rec_ref, table_ref, valid_ref, out_ref):
    station_count, window_count = valid_ref.shape
    comp_count = rec_ref.shape[0] // station_count
    nb = table_ref.shape[0] // 2
    table = table_ref[...]
    zero_row = jnp.zeros((1, window_count), jnp.float32)
    for s in range(station_count):
        parts = []
        for c in range(comp_count):
            z = lax.dot_general(
                table,
                rec_ref[c * station_count + s],
                (((1,), (1,)), ((), ())),
                preferred_element_type=jnp.float32,
            )
            parts.append((z[:nb], z[nb:]))
        total = parts[0][0] * parts[0][0] + parts[0][1] * parts[0][1]
        for c in range(1, comp_count):
            total = total + (parts[c][0] * parts[c][0] + parts[c][1] * parts[c][1])
        band_power = total / float(comp_count)
        amplitude = jnp.sqrt(jnp.maximum(band_power, 0.25))
        valid_row = valid_ref[pl.ds(s, 1), :]
        factor = valid_row / amplitude
        for c in range(comp_count):
            x = c * station_count + s
            out_ref[x, pl.ds(0, 1), pl.ds(0, window_count)] = valid_row if c == 0 else zero_row
            out_ref[x, pl.ds(0, 1), pl.ds(window_count, window_count)] = zero_row
            out_ref[x, pl.ds(1, nb), pl.ds(0, window_count)] = parts[c][0] * factor
            out_ref[x, pl.ds(1, nb), pl.ds(window_count, window_count)] = parts[c][1] * factor


def dft_whiten(rec_t, table_t, valid_t):
    rows, window_count, sample_points = rec_t.shape
    nb = table_t.shape[0] // 2
    return pl.pallas_call(
        dft_kernel,
        out_shape=jax.ShapeDtypeStruct((rows, 1 + nb, 2 * window_count), jnp.float32),
        cost_estimate=pl.CostEstimate(
            flops=2 * rows * window_count * sample_points * 2 * nb,
            transcendentals=rows * nb * window_count,
            bytes_accessed=2 * rec_t.size + 2 * table_t.size + 4 * rows * (nb + 1) * 2 * window_count,
        ),
    )(rec_t, table_t, valid_t)


def exchange(prod, station_count, bands, band_index):
    group = lax.axis_size("win") * bands
    per_dev = station_count // group
    me = lax.axis_index("win") * bands + band_index
    by_offset = [None] * bands
    for shift in range(group):
        dest = (me + shift) % group
        chunk = lax.dynamic_slice_in_dim(prod, dest * per_dev, per_dev, 2)
        if shift:
            perm = [(k, (k + shift) % group) for k in range(group)]
            chunk = lax.ppermute(chunk.astype(jnp.bfloat16), ("win", "band"), perm)
            chunk = chunk.astype(jnp.float32)
        q = shift % bands
        by_offset[q] = chunk if by_offset[q] is None else by_offset[q] + chunk
    ordered = []
    for bb in range(bands):
        pick = by_offset[0]
        for q in range(1, bands):
            pick = jnp.where((band_index - q) % bands == bb, by_offset[q], pick)
        ordered.append(pick)
    return jnp.stack(ordered, axis=0), by_offset[0]


def body(records, valid_mask, round_keys):
    window_count, comp_count, station_count, sample_points = records.shape
    bands = lax.axis_size("band")
    band_index = lax.axis_index("band")
    pair_index = lax.axis_index("pair")
    nb = FREQ // bands
    rounds = round_keys.shape[0]
    xs = comp_count * station_count
    lanes = 2 * window_count
    slots = nb + 1

    dft_rows = dft_table(sample_points, nb, band_index * nb)
    rec_t = records.reshape(window_count, xs, sample_points).transpose(1, 0, 2)
    validity = valid_mask.astype(jnp.float32)
    spec = dft_whiten(rec_t, dft_rows.T, validity.T).astype(jnp.bfloat16)

    flat = spec.reshape(xs * slots, lanes)
    blocks = lax.axis_size("pair")
    if blocks <= 8 and blocks & (blocks - 1) == 0:
        held = [flat]
        for k in range(1, blocks):
            held.append(lax.ppermute(flat, "pair", [(p, p ^ k) for p in range(blocks)]))
        other = jnp.take(jnp.stack(held), round_keys, axis=0, mode="clip")
    else:
        gathered = lax.all_gather(flat, "pair", axis=0, tiled=False)
        partner_list = jnp.bitwise_xor(pair_index, round_keys)
        other = jnp.take(gathered, partner_list, axis=0, mode="clip")
    other = other.reshape(rounds, xs, slots, lanes)
    rhs = other.transpose(2, 0, 1, 3).reshape(slots, rounds * xs, lanes)

    half = lax.broadcasted_iota(jnp.int32, (lanes,), 0) < window_count
    turned = jnp.roll(spec, window_count, axis=-1) * jnp.where(half, 1.0, -1.0).astype(jnp.bfloat16)
    lhs = jnp.stack([spec, turned], axis=0).transpose(2, 0, 1, 3).reshape(slots, 2 * xs, lanes)
    prod = jnp.einsum("fxk,fyk->fxy", lhs, rhs, preferred_element_type=jnp.float32)
    prod = prod.reshape(slots, 2 * comp_count, station_count, rounds * xs)

    stacked, same = exchange(prod, station_count, bands, band_index)
    per_dev = stacked.shape[3]
    totals = same[0, 0].reshape(per_dev, rounds, comp_count, station_count)[:, :, 0, :]
    stacked = stacked[:, 1:].reshape(
        bands, nb, 2, comp_count, per_dev, rounds, comp_count, station_count
    )

    full_lag = lag_table(sample_points, FREQ, 0, NLAG, FREQ)
    full_lag = full_lag.reshape(2, bands, nb, NLAG).transpose(1, 0, 2, 3)
    lagged = jnp.einsum(
        "gfuairbj,gufl->riabjl",
        stacked,
        full_lag,
        precision=lax.Precision.HIGHEST,
        preferred_element_type=jnp.float32,
    )
    divisor = jnp.maximum(totals, 1.0).transpose(1, 0, 2)[:, :, None, None, :, None]
    lagged = lagged / divisor
    return lagged.reshape(rounds, per_dev, comp_count, comp_count * station_count, NLAG)


def solution(mesh):
    placed = (P(("hours", "win"), None, "pair", None), P(("hours", "win"), "pair"), P())
    return jax.shard_map(
        body,
        mesh=mesh,
        in_specs=placed,
        out_specs=P(None, ("hours", "pair", "win", "band"), None, None, None),
        check_vma=False,
    )
```

```python
import math

import jax
import jax.numpy as jnp
from jax import lax
from jax.experimental import pallas as pl
from jax.experimental.pallas import tpu as pltpu
from jax.sharding import PartitionSpec as P

FREQ = 128
NLAG = 256
ROUNDS = 4
WSTEP = 4


def dft_table(sample_points, bin_count, first_bin):
    sample_moments = jnp.arange(sample_points, dtype=jnp.int32)
    spectral_bin_index = first_bin + 1 + jnp.arange(bin_count, dtype=jnp.int32)
    phase_turns = jnp.mod(sample_moments[:, None] * spectral_bin_index[None, :], sample_points)
    phases = phase_turns.astype(jnp.float32) * (2.0 * math.pi / sample_points)
    hanning_taper = 0.5 - 0.5 * jnp.cos(
        sample_moments.astype(jnp.float32) * (2.0 * math.pi / sample_points)
    )
    weight = (hanning_taper * math.sqrt(8.0 / (3.0 * sample_points)))[:, None]
    return jnp.concatenate([weight * jnp.cos(phases), -(weight * jnp.sin(phases))], axis=1).astype(
        jnp.bfloat16
    )


def lag_table(sample_points, bin_count, first_bin, lag_count, all_bins):
    spectral_bin_index = first_bin + 1 + jnp.arange(bin_count, dtype=jnp.int32)
    shifts = jnp.arange(lag_count, dtype=jnp.int32) - lag_count // 2
    phase_turns = jnp.mod(spectral_bin_index[:, None] * shifts[None, :], sample_points)
    phases = phase_turns.astype(jnp.float32) * (2.0 * math.pi / sample_points)
    lag_scale = 1.0 / math.sqrt(all_bins)
    return jnp.concatenate([jnp.cos(phases) * lag_scale, -(jnp.sin(phases) * lag_scale)], axis=0)


def whiten(spectra, validity):
    bin_count = spectra.shape[-1] // 2
    real_part = spectra[..., :bin_count]
    imag_part = spectra[..., bin_count:]
    band_power = jnp.mean(real_part * real_part + imag_part * imag_part, axis=1)
    amplitude = jnp.sqrt(jnp.maximum(band_power, 0.25))
    factor = validity[:, :, None] / amplitude
    factor = jnp.concatenate([factor, factor], axis=-1)
    return (spectra * factor[:, None]).astype(jnp.bfloat16)


def dft_kernel(rec_ref, table_ref, valid_ref, out_ref):
    station_count, window_count = valid_ref.shape
    comp_count = rec_ref.shape[0] // station_count
    nb = table_ref.shape[0] // 2
    table = table_ref[...]
    zero_row = jnp.zeros((1, window_count), jnp.float32)
    for s in range(station_count):
        parts = []
        for c in range(comp_count):
            z = lax.dot_general(
                table,
                rec_ref[c * station_count + s],
                (((1,), (1,)), ((), ())),
                preferred_element_type=jnp.float32,
            )
            parts.append((z[:nb], z[nb:]))
        total = parts[0][0] * parts[0][0] + parts[0][1] * parts[0][1]
        for c in range(1, comp_count):
            total = total + (parts[c][0] * parts[c][0] + parts[c][1] * parts[c][1])
        band_power = total / float(comp_count)
        amplitude = jnp.sqrt(jnp.maximum(band_power, 0.25))
        valid_row = valid_ref[pl.ds(s, 1), :]
        factor = valid_row / amplitude
        for c in range(comp_count):
            x = c * station_count + s
            out_ref[x, pl.ds(0, 1), pl.ds(0, window_count)] = valid_row if c == 0 else zero_row
            out_ref[x, pl.ds(0, 1), pl.ds(window_count, window_count)] = zero_row
            out_ref[x, pl.ds(1, nb), pl.ds(0, window_count)] = parts[c][0] * factor
            out_ref[x, pl.ds(1, nb), pl.ds(window_count, window_count)] = parts[c][1] * factor


def dft_whiten(rec_t, table_t, valid_t):
    rows, window_count, sample_points = rec_t.shape
    nb = table_t.shape[0] // 2
    return pl.pallas_call(
        dft_kernel,
        out_shape=jax.ShapeDtypeStruct((rows, 1 + nb, 2 * window_count), jnp.float32),
        cost_estimate=pl.CostEstimate(
            flops=2 * rows * window_count * sample_points * 2 * nb,
            transcendentals=rows * nb * window_count,
            bytes_accessed=2 * rec_t.size + 2 * table_t.size + 4 * rows * (nb + 1) * 2 * window_count,
        ),
    )(rec_t, table_t, valid_t)


def exchange(prod, station_count, bands, band_index):
    group = lax.axis_size("win") * bands
    per_dev = station_count // group
    me = lax.axis_index("win") * bands + band_index
    by_offset = [None] * bands
    for shift in range(group):
        dest = (me + shift) % group
        chunk = lax.dynamic_slice_in_dim(prod, dest * per_dev, per_dev, 2)
        if shift:
            perm = [(k, (k + shift) % group) for k in range(group)]
            chunk = lax.ppermute(chunk.astype(jnp.bfloat16), ("win", "band"), perm)
            chunk = chunk.astype(jnp.float32)
        q = shift % bands
        by_offset[q] = chunk if by_offset[q] is None else by_offset[q] + chunk
    ordered = []
    for bb in range(bands):
        pick = by_offset[0]
        for q in range(1, bands):
            pick = jnp.where((band_index - q) % bands == bb, by_offset[q], pick)
        ordered.append(pick)
    return jnp.stack(ordered, axis=0), by_offset[0]


def body(records, valid_mask, round_keys):
    window_count, comp_count, station_count, sample_points = records.shape
    bands = lax.axis_size("band")
    band_index = lax.axis_index("band")
    pair_index = lax.axis_index("pair")
    nb = FREQ // bands
    rounds = round_keys.shape[0]
    xs = comp_count * station_count
    lanes = 2 * window_count
    slots = nb + 1

    dft_rows = dft_table(sample_points, nb, band_index * nb)
    rec_t = records.reshape(window_count, xs, sample_points).transpose(1, 0, 2)
    validity = valid_mask.astype(jnp.float32)
    spec = dft_whiten(rec_t, dft_rows.T, validity.T).astype(jnp.bfloat16)

    flat = spec.reshape(xs * slots, lanes)
    blocks = lax.axis_size("pair")

    half = lax.broadcasted_iota(jnp.int32, (lanes,), 0) < window_count
    turned = jnp.roll(spec, window_count, axis=-1) * jnp.where(half, 1.0, -1.0).astype(jnp.bfloat16)
    lhs = jnp.stack([spec, turned], axis=0).transpose(2, 0, 1, 3).reshape(slots, 2 * xs, lanes)

    def cross_with(other):
        count = other.shape[0]
        rhs = other.transpose(2, 0, 1, 3).reshape(slots, count * xs, lanes)
        prod = jnp.einsum("fxk,fyk->fxy", lhs, rhs, preferred_element_type=jnp.float32)
        prod = prod.reshape(slots, 2 * comp_count, station_count, count * xs)
        stacked, same = exchange(prod, station_count, bands, band_index)
        per_dev = stacked.shape[3]
        totals = same[0, 0].reshape(per_dev, count, comp_count, station_count)[:, :, 0, :]
        stacked = stacked.reshape(bands, slots, 2 * comp_count, per_dev, count, xs)
        return stacked, totals

    if blocks <= 8 and blocks & (blocks - 1) == 0:
        outs, tots = [], []
        for k in range(blocks):
            held = flat
            if k:
                held = lax.ppermute(flat, "pair", [(p, p ^ k) for p in range(blocks)])
            st, to = cross_with(held.reshape(1, xs, slots, lanes))
            outs.append(st[..., 0, :])
            tots.append(to[:, 0])
        chosen = jnp.take(jnp.stack(outs), round_keys, axis=0, mode="clip")
        totals = jnp.take(jnp.stack(tots), round_keys, axis=0, mode="clip")
        chosen = jnp.moveaxis(chosen, 0, -2)
    else:
        gathered = lax.all_gather(flat, "pair", axis=0, tiled=False)
        partner_list = jnp.bitwise_xor(pair_index, round_keys)
        other = jnp.take(gathered, partner_list, axis=0, mode="clip").reshape(rounds, xs, slots, lanes)
        chosen, totals = cross_with(other)
        totals = totals.transpose(1, 0, 2)
    per_dev = chosen.shape[3]
    stacked = chosen[:, 1:].reshape(
        bands, nb, 2, comp_count, per_dev, rounds, comp_count, station_count
    )

    full_lag = lag_table(sample_points, FREQ, 0, NLAG, FREQ)
    full_lag = full_lag.reshape(2, bands, nb, NLAG).transpose(1, 0, 2, 3)
    lagged = jnp.einsum(
        "gfuairbj,gufl->riabjl",
        stacked,
        full_lag,
        precision=lax.Precision.HIGHEST,
        preferred_element_type=jnp.float32,
    )
    divisor = jnp.maximum(totals, 1.0)[:, :, None, None, :, None]
    lagged = lagged / divisor
    return lagged.reshape(rounds, per_dev, comp_count, comp_count * station_count, NLAG)


def solution(mesh):
    placed = (P(("hours", "win"), None, "pair", None), P(("hours", "win"), "pair"), P())
    return jax.shard_map(
        body,
        mesh=mesh,
        in_specs=placed,
        out_specs=P(None, ("hours", "pair", "win", "band"), None, None, None),
        check_vma=False,
    )
```

```python
import math

import jax
import jax.numpy as jnp
from jax import lax
from jax.experimental import pallas as pl
from jax.experimental.pallas import tpu as pltpu
from jax.sharding import PartitionSpec as P

FREQ = 128
NLAG = 256
ROUNDS = 4
WSTEP = 4


def dft_table(sample_points, bin_count, first_bin):
    sample_moments = jnp.arange(sample_points, dtype=jnp.int32)
    spectral_bin_index = first_bin + 1 + jnp.arange(bin_count, dtype=jnp.int32)
    phase_turns = jnp.mod(sample_moments[:, None] * spectral_bin_index[None, :], sample_points)
    phases = phase_turns.astype(jnp.float32) * (2.0 * math.pi / sample_points)
    hanning_taper = 0.5 - 0.5 * jnp.cos(
        sample_moments.astype(jnp.float32) * (2.0 * math.pi / sample_points)
    )
    weight = (hanning_taper * math.sqrt(8.0 / (3.0 * sample_points)))[:, None]
    return jnp.concatenate([weight * jnp.cos(phases), -(weight * jnp.sin(phases))], axis=1).astype(
        jnp.bfloat16
    )


def lag_table(sample_points, bin_count, first_bin, lag_count, all_bins):
    spectral_bin_index = first_bin + 1 + jnp.arange(bin_count, dtype=jnp.int32)
    shifts = jnp.arange(lag_count, dtype=jnp.int32) - lag_count // 2
    phase_turns = jnp.mod(spectral_bin_index[:, None] * shifts[None, :], sample_points)
    phases = phase_turns.astype(jnp.float32) * (2.0 * math.pi / sample_points)
    lag_scale = 1.0 / math.sqrt(all_bins)
    return jnp.concatenate([jnp.cos(phases) * lag_scale, -(jnp.sin(phases) * lag_scale)], axis=0)


def whiten(spectra, validity):
    bin_count = spectra.shape[-1] // 2
    real_part = spectra[..., :bin_count]
    imag_part = spectra[..., bin_count:]
    band_power = jnp.mean(real_part * real_part + imag_part * imag_part, axis=1)
    amplitude = jnp.sqrt(jnp.maximum(band_power, 0.25))
    factor = validity[:, :, None] / amplitude
    factor = jnp.concatenate([factor, factor], axis=-1)
    return (spectra * factor[:, None]).astype(jnp.bfloat16)


def dft_kernel(rec_ref, table_ref, valid_ref, out_ref):
    station_count, window_count = valid_ref.shape
    comp_count = rec_ref.shape[0] // station_count
    nb = table_ref.shape[0] // 2
    table = table_ref[...]
    zero_row = jnp.zeros((1, window_count), jnp.float32)
    for s in range(station_count):
        parts = []
        for c in range(comp_count):
            z = lax.dot_general(
                table,
                rec_ref[c * station_count + s],
                (((1,), (1,)), ((), ())),
                preferred_element_type=jnp.float32,
            )
            parts.append((z[:nb], z[nb:]))
        total = parts[0][0] * parts[0][0] + parts[0][1] * parts[0][1]
        for c in range(1, comp_count):
            total = total + (parts[c][0] * parts[c][0] + parts[c][1] * parts[c][1])
        band_power = total / float(comp_count)
        amplitude = jnp.sqrt(jnp.maximum(band_power, 0.25))
        valid_row = valid_ref[pl.ds(s, 1), :]
        factor = valid_row / amplitude
        for c in range(comp_count):
            x = c * station_count + s
            out_ref[x, pl.ds(0, 1), pl.ds(0, window_count)] = valid_row if c == 0 else zero_row
            out_ref[x, pl.ds(0, 1), pl.ds(window_count, window_count)] = zero_row
            out_ref[x, pl.ds(1, nb), pl.ds(0, window_count)] = parts[c][0] * factor
            out_ref[x, pl.ds(1, nb), pl.ds(window_count, window_count)] = parts[c][1] * factor


def dft_whiten(rec_t, table_t, valid_t):
    rows, window_count, sample_points = rec_t.shape
    nb = table_t.shape[0] // 2
    return pl.pallas_call(
        dft_kernel,
        out_shape=jax.ShapeDtypeStruct((rows, 1 + nb, 2 * window_count), jnp.float32),
        cost_estimate=pl.CostEstimate(
            flops=2 * rows * window_count * sample_points * 2 * nb,
            transcendentals=rows * nb * window_count,
            bytes_accessed=2 * rec_t.size + 2 * table_t.size + 4 * rows * (nb + 1) * 2 * window_count,
        ),
    )(rec_t, table_t, valid_t)


def exchange(prod, station_count, bands, band_index):
    group = lax.axis_size("win") * bands
    per_dev = station_count // group
    me = lax.axis_index("win") * bands + band_index
    by_offset = [None] * bands
    for shift in range(group):
        dest = (me + shift) % group
        chunk = lax.dynamic_slice_in_dim(prod, dest * per_dev, per_dev, 2)
        if shift:
            perm = [(k, (k + shift) % group) for k in range(group)]
            chunk = lax.ppermute(chunk.astype(jnp.bfloat16), ("win", "band"), perm)
            chunk = chunk.astype(jnp.float32)
        q = shift % bands
        by_offset[q] = chunk if by_offset[q] is None else by_offset[q] + chunk
    ordered = []
    for bb in range(bands):
        pick = by_offset[0]
        for q in range(1, bands):
            pick = jnp.where((band_index - q) % bands == bb, by_offset[q], pick)
        ordered.append(pick)
    return jnp.stack(ordered, axis=0), by_offset[0]


def body(records, valid_mask, round_keys):
    window_count, comp_count, station_count, sample_points = records.shape
    bands = lax.axis_size("band")
    band_index = lax.axis_index("band")
    pair_index = lax.axis_index("pair")
    nb = FREQ // bands
    rounds = round_keys.shape[0]
    xs = comp_count * station_count
    lanes = 2 * window_count
    slots = nb + 1

    dft_rows = dft_table(sample_points, nb, band_index * nb)
    rec_t = records.reshape(window_count, xs, sample_points).transpose(1, 0, 2)
    validity = valid_mask.astype(jnp.float32)
    spec = dft_whiten(rec_t, dft_rows.T, validity.T).astype(jnp.bfloat16)

    flat = spec.reshape(xs * slots, lanes)
    blocks = lax.axis_size("pair")

    half = lax.broadcasted_iota(jnp.int32, (lanes,), 0) < window_count
    turned = jnp.roll(spec, window_count, axis=-1) * jnp.where(half, 1.0, -1.0).astype(jnp.bfloat16)
    lhs = jnp.stack([spec, turned], axis=0).transpose(2, 0, 1, 3).reshape(slots, 2 * xs, lanes)

    def cross_with(other):
        count = other.shape[0]
        rhs = other.transpose(2, 0, 1, 3).reshape(slots, count * xs, lanes)
        prod = jnp.einsum("fxk,fyk->fxy", lhs, rhs, preferred_element_type=jnp.float32)
        prod = prod.reshape(slots, 2 * comp_count, station_count, count * xs)
        stacked, same = exchange(prod, station_count, bands, band_index)
        per_dev = stacked.shape[3]
        totals = same[0, 0].reshape(per_dev, count, comp_count, station_count)[:, :, 0, :]
        stacked = stacked.reshape(bands, slots, 2 * comp_count, per_dev, count, xs)
        return stacked, totals

    if blocks <= 8 and blocks & (blocks - 1) == 0:
        held = [flat] + [
            lax.ppermute(flat, "pair", [(p, p ^ k) for p in range(blocks)]) for k in range(1, blocks)
        ]
        groups = [[0], [1], list(range(2, blocks))] if blocks > 2 else [[k] for k in range(blocks)]
        outs, tots = [], []
        for members in groups:
            other = jnp.stack([held[k] for k in members]).reshape(len(members), xs, slots, lanes)
            st, to = cross_with(other)
            for n in range(len(members)):
                outs.append(st[..., n, :])
                tots.append(to[:, n])
        chosen = jnp.take(jnp.stack(outs), round_keys, axis=0, mode="clip")
        totals = jnp.take(jnp.stack(tots), round_keys, axis=0, mode="clip")
        chosen = jnp.moveaxis(chosen, 0, -2)
    else:
        gathered = lax.all_gather(flat, "pair", axis=0, tiled=False)
        partner_list = jnp.bitwise_xor(pair_index, round_keys)
        other = jnp.take(gathered, partner_list, axis=0, mode="clip").reshape(rounds, xs, slots, lanes)
        chosen, totals = cross_with(other)
        totals = totals.transpose(1, 0, 2)
    per_dev = chosen.shape[3]
    stacked = chosen[:, 1:].reshape(
        bands, nb, 2, comp_count, per_dev, rounds, comp_count, station_count
    )

    full_lag = lag_table(sample_points, FREQ, 0, NLAG, FREQ)
    full_lag = full_lag.reshape(2, bands, nb, NLAG).transpose(1, 0, 2, 3)
    lagged = jnp.einsum(
        "gfuairbj,gufl->riabjl",
        stacked,
        full_lag,
        precision=lax.Precision.HIGHEST,
        preferred_element_type=jnp.float32,
    )
    divisor = jnp.maximum(totals, 1.0)[:, :, None, None, :, None]
    lagged = lagged / divisor
    return lagged.reshape(rounds, per_dev, comp_count, comp_count * station_count, NLAG)


def solution(mesh):
    placed = (P(("hours", "win"), None, "pair", None), P(("hours", "win"), "pair"), P())
    return jax.shard_map(
        body,
        mesh=mesh,
        in_specs=placed,
        out_specs=P(None, ("hours", "pair", "win", "band"), None, None, None),
        check_vma=False,
    )
```

```python
import math

import jax
import jax.numpy as jnp
from jax import lax
from jax.experimental import pallas as pl
from jax.experimental.pallas import tpu as pltpu
from jax.sharding import PartitionSpec as P

FREQ = 128
NLAG = 256
ROUNDS = 4
WSTEP = 4


def dft_table(sample_points, bin_count, first_bin):
    sample_moments = jnp.arange(sample_points, dtype=jnp.int32)
    spectral_bin_index = first_bin + 1 + jnp.arange(bin_count, dtype=jnp.int32)
    phase_turns = jnp.mod(sample_moments[:, None] * spectral_bin_index[None, :], sample_points)
    phases = phase_turns.astype(jnp.float32) * (2.0 * math.pi / sample_points)
    hanning_taper = 0.5 - 0.5 * jnp.cos(
        sample_moments.astype(jnp.float32) * (2.0 * math.pi / sample_points)
    )
    weight = (hanning_taper * math.sqrt(8.0 / (3.0 * sample_points)))[:, None]
    return jnp.concatenate([weight * jnp.cos(phases), -(weight * jnp.sin(phases))], axis=1).astype(
        jnp.bfloat16
    )


def lag_table(sample_points, bin_count, first_bin, lag_count, all_bins):
    spectral_bin_index = first_bin + 1 + jnp.arange(bin_count, dtype=jnp.int32)
    shifts = jnp.arange(lag_count, dtype=jnp.int32) - lag_count // 2
    phase_turns = jnp.mod(spectral_bin_index[:, None] * shifts[None, :], sample_points)
    phases = phase_turns.astype(jnp.float32) * (2.0 * math.pi / sample_points)
    lag_scale = 1.0 / math.sqrt(all_bins)
    return jnp.concatenate([jnp.cos(phases) * lag_scale, -(jnp.sin(phases) * lag_scale)], axis=0)


def whiten(spectra, validity):
    bin_count = spectra.shape[-1] // 2
    real_part = spectra[..., :bin_count]
    imag_part = spectra[..., bin_count:]
    band_power = jnp.mean(real_part * real_part + imag_part * imag_part, axis=1)
    amplitude = jnp.sqrt(jnp.maximum(band_power, 0.25))
    factor = validity[:, :, None] / amplitude
    factor = jnp.concatenate([factor, factor], axis=-1)
    return (spectra * factor[:, None]).astype(jnp.bfloat16)


def dft_kernel(rec_ref, table_ref, valid_ref, out_ref):
    station_count, window_count = valid_ref.shape
    comp_count = rec_ref.shape[0] // station_count
    nb = table_ref.shape[0] // 2
    table = table_ref[...]
    zero_row = jnp.zeros((1, window_count), jnp.float32)
    for s in range(station_count):
        parts = []
        for c in range(comp_count):
            z = lax.dot_general(
                table,
                rec_ref[c * station_count + s],
                (((1,), (1,)), ((), ())),
                preferred_element_type=jnp.float32,
            )
            parts.append((z[:nb], z[nb:]))
        total = parts[0][0] * parts[0][0] + parts[0][1] * parts[0][1]
        for c in range(1, comp_count):
            total = total + (parts[c][0] * parts[c][0] + parts[c][1] * parts[c][1])
        band_power = total / float(comp_count)
        amplitude = jnp.sqrt(jnp.maximum(band_power, 0.25))
        valid_row = valid_ref[pl.ds(s, 1), :]
        factor = valid_row / amplitude
        for c in range(comp_count):
            x = c * station_count + s
            out_ref[x, pl.ds(0, 1), pl.ds(0, window_count)] = valid_row if c == 0 else zero_row
            out_ref[x, pl.ds(0, 1), pl.ds(window_count, window_count)] = zero_row
            out_ref[x, pl.ds(1, nb), pl.ds(0, window_count)] = parts[c][0] * factor
            out_ref[x, pl.ds(1, nb), pl.ds(window_count, window_count)] = parts[c][1] * factor


def dft_whiten(rec_t, table_t, valid_t):
    rows, window_count, sample_points = rec_t.shape
    nb = table_t.shape[0] // 2
    return pl.pallas_call(
        dft_kernel,
        out_shape=jax.ShapeDtypeStruct((rows, 1 + nb, 2 * window_count), jnp.float32),
        cost_estimate=pl.CostEstimate(
            flops=2 * rows * window_count * sample_points * 2 * nb,
            transcendentals=rows * nb * window_count,
            bytes_accessed=2 * rec_t.size + 2 * table_t.size + 4 * rows * (nb + 1) * 2 * window_count,
        ),
    )(rec_t, table_t, valid_t)


def exchange(prod, station_count, bands, band_index):
    wins = lax.axis_size("win")
    group = wins * bands
    per_dev = station_count // group
    slots, rows, _, ys = prod.shape
    parts = prod.reshape(slots, rows, group, per_dev, ys)
    parts = jnp.moveaxis(parts, 2, 0).astype(jnp.bfloat16)
    got = lax.all_to_all(parts, ("win", "band"), split_axis=0, concat_axis=0, tiled=True)
    got = got.astype(jnp.float32).reshape(wins, bands, slots, rows, per_dev, ys).sum(axis=0)
    return got, got[0]


def body(records, valid_mask, round_keys):
    window_count, comp_count, station_count, sample_points = records.shape
    bands = lax.axis_size("band")
    band_index = lax.axis_index("band")
    pair_index = lax.axis_index("pair")
    nb = FREQ // bands
    rounds = round_keys.shape[0]
    xs = comp_count * station_count
    lanes = 2 * window_count
    slots = nb + 1

    dft_rows = dft_table(sample_points, nb, band_index * nb)
    rec_t = records.reshape(window_count, xs, sample_points).transpose(1, 0, 2)
    validity = valid_mask.astype(jnp.float32)
    spec = dft_whiten(rec_t, dft_rows.T, validity.T).astype(jnp.bfloat16)

    flat = spec.reshape(xs * slots, lanes)
    blocks = lax.axis_size("pair")

    half = lax.broadcasted_iota(jnp.int32, (lanes,), 0) < window_count
    turned = jnp.roll(spec, window_count, axis=-1) * jnp.where(half, 1.0, -1.0).astype(jnp.bfloat16)
    lhs = jnp.stack([spec, turned], axis=0).transpose(2, 0, 1, 3).reshape(slots, 2 * xs, lanes)

    def cross_with(other):
        count = other.shape[0]
        rhs = other.transpose(2, 0, 1, 3).reshape(slots, count * xs, lanes)
        prod = jnp.einsum("fxk,fyk->fxy", lhs, rhs, preferred_element_type=jnp.float32)
        prod = prod.reshape(slots, 2 * comp_count, station_count, count * xs)
        stacked, same = exchange(prod, station_count, bands, band_index)
        per_dev = stacked.shape[3]
        totals = same[0, 0].reshape(per_dev, count, comp_count, station_count)[:, :, 0, :]
        stacked = stacked.reshape(bands, slots, 2 * comp_count, per_dev, count, xs)
        return stacked, totals

    if blocks <= 8 and blocks & (blocks - 1) == 0:
        outs, tots = [], []
        for k in range(blocks):
            held = flat
            if k:
                held = lax.ppermute(flat, "pair", [(p, p ^ k) for p in range(blocks)])
            st, to = cross_with(held.reshape(1, xs, slots, lanes))
            outs.append(st[..., 0, :])
            tots.append(to[:, 0])
        chosen = jnp.take(jnp.stack(outs), round_keys, axis=0, mode="clip")
        totals = jnp.take(jnp.stack(tots), round_keys, axis=0, mode="clip")
        chosen = jnp.moveaxis(chosen, 0, -2)
    else:
        gathered = lax.all_gather(flat, "pair", axis=0, tiled=False)
        partner_list = jnp.bitwise_xor(pair_index, round_keys)
        other = jnp.take(gathered, partner_list, axis=0, mode="clip").reshape(rounds, xs, slots, lanes)
        chosen, totals = cross_with(other)
        totals = totals.transpose(1, 0, 2)
    per_dev = chosen.shape[3]
    stacked = chosen[:, 1:].reshape(
        bands, nb, 2, comp_count, per_dev, rounds, comp_count, station_count
    )

    full_lag = lag_table(sample_points, FREQ, 0, NLAG, FREQ)
    full_lag = full_lag.reshape(2, bands, nb, NLAG).transpose(1, 0, 2, 3)
    lagged = jnp.einsum(
        "gfuairbj,gufl->riabjl",
        stacked,
        full_lag,
        precision=lax.Precision.HIGHEST,
        preferred_element_type=jnp.float32,
    )
    divisor = jnp.maximum(totals, 1.0)[:, :, None, None, :, None]
    lagged = lagged / divisor
    return lagged.reshape(rounds, per_dev, comp_count, comp_count * station_count, NLAG)


def solution(mesh):
    placed = (P(("hours", "win"), None, "pair", None), P(("hours", "win"), "pair"), P())
    return jax.shard_map(
        body,
        mesh=mesh,
        in_specs=placed,
        out_specs=P(None, ("hours", "pair", "win", "band"), None, None, None),
        check_vma=False,
    )
```

```python
import math

import jax
import jax.numpy as jnp
from jax import lax
from jax.experimental import pallas as pl
from jax.sharding import PartitionSpec as P


FREQ = 128
NLAG = 256


def dft_table(sample_points, bin_count, first_bin):
    sample_moments = jnp.arange(sample_points, dtype=jnp.int32)
    spectral_bin_index = first_bin + 1 + jnp.arange(bin_count, dtype=jnp.int32)
    phase_turns = jnp.mod(sample_moments[:, None] * spectral_bin_index[None, :], sample_points)
    phases = phase_turns.astype(jnp.float32) * (2.0 * math.pi / sample_points)
    hanning_taper = 0.5 - 0.5 * jnp.cos(
        sample_moments.astype(jnp.float32) * (2.0 * math.pi / sample_points)
    )
    weight = (hanning_taper * math.sqrt(8.0 / (3.0 * sample_points)))[:, None]
    return jnp.concatenate([weight * jnp.cos(phases), -(weight * jnp.sin(phases))], axis=1).astype(
        jnp.bfloat16
    )


def lag_table(sample_points, bin_count, first_bin, lag_count, all_bins):
    spectral_bin_index = first_bin + 1 + jnp.arange(bin_count, dtype=jnp.int32)
    shifts = jnp.arange(lag_count, dtype=jnp.int32) - lag_count // 2
    phase_turns = jnp.mod(spectral_bin_index[:, None] * shifts[None, :], sample_points)
    phases = phase_turns.astype(jnp.float32) * (2.0 * math.pi / sample_points)
    lag_scale = 1.0 / math.sqrt(all_bins)
    return jnp.concatenate([jnp.cos(phases) * lag_scale, -(jnp.sin(phases) * lag_scale)], axis=0)


def dft_kernel(rec_ref, table_ref, valid_ref, out_ref):
    station_count, window_count = valid_ref.shape
    comp_count = rec_ref.shape[0] // station_count
    nb = table_ref.shape[0] // 2
    table = table_ref[...]
    zero_row = jnp.zeros((1, window_count), jnp.float32)
    for s in range(station_count):
        parts = []
        for c in range(comp_count):
            z = lax.dot_general(
                table,
                rec_ref[c * station_count + s],
                (((1,), (1,)), ((), ())),
                preferred_element_type=jnp.float32,
            )
            parts.append((z[:nb], z[nb:]))
        total = parts[0][0] * parts[0][0] + parts[0][1] * parts[0][1]
        for c in range(1, comp_count):
            total = total + (parts[c][0] * parts[c][0] + parts[c][1] * parts[c][1])
        band_power = total / float(comp_count)
        amplitude = jnp.sqrt(jnp.maximum(band_power, 0.25))
        valid_row = valid_ref[pl.ds(s, 1), :]
        factor = valid_row / amplitude
        for c in range(comp_count):
            x = c * station_count + s
            out_ref[x, pl.ds(0, 1), pl.ds(0, window_count)] = valid_row if c == 0 else zero_row
            out_ref[x, pl.ds(0, 1), pl.ds(window_count, window_count)] = zero_row
            out_ref[x, pl.ds(1, nb), pl.ds(0, window_count)] = parts[c][0] * factor
            out_ref[x, pl.ds(1, nb), pl.ds(window_count, window_count)] = parts[c][1] * factor


def dft_whiten(rec_t, table_t, valid_t):
    rows, window_count, sample_points = rec_t.shape
    nb = table_t.shape[0] // 2
    return pl.pallas_call(
        dft_kernel,
        out_shape=jax.ShapeDtypeStruct((rows, 1 + nb, 2 * window_count), jnp.float32),
        cost_estimate=pl.CostEstimate(
            flops=2 * rows * window_count * sample_points * 2 * nb,
            transcendentals=rows * nb * window_count,
            bytes_accessed=2 * rec_t.size + 2 * table_t.size + 4 * rows * (nb + 1) * 2 * window_count,
        ),
    )(rec_t, table_t, valid_t)


def exchange(prod, station_count, bands, band_index):
    group = lax.axis_size("win") * bands
    per_dev = station_count // group
    me = lax.axis_index("win") * bands + band_index
    by_offset = [None] * bands
    for shift in range(group):
        dest = (me + shift) % group
        chunk = lax.dynamic_slice_in_dim(prod, dest * per_dev, per_dev, 2)
        if shift:
            perm = [(k, (k + shift) % group) for k in range(group)]
            chunk = lax.ppermute(chunk.astype(jnp.bfloat16), ("win", "band"), perm)
            chunk = chunk.astype(jnp.float32)
        q = shift % bands
        by_offset[q] = chunk if by_offset[q] is None else by_offset[q] + chunk
    ordered = []
    for bb in range(bands):
        pick = by_offset[0]
        for q in range(1, bands):
            pick = jnp.where((band_index - q) % bands == bb, by_offset[q], pick)
        ordered.append(pick)
    return jnp.stack(ordered, axis=0), by_offset[0]


def body(records, valid_mask, round_keys):
    window_count, comp_count, station_count, sample_points = records.shape
    bands = lax.axis_size("band")
    band_index = lax.axis_index("band")
    pair_index = lax.axis_index("pair")
    nb = FREQ // bands
    rounds = round_keys.shape[0]
    xs = comp_count * station_count
    lanes = 2 * window_count
    slots = nb + 1

    dft_rows = dft_table(sample_points, nb, band_index * nb)
    rec_t = records.reshape(window_count, xs, sample_points).transpose(1, 0, 2)
    validity = valid_mask.astype(jnp.float32)
    spec = dft_whiten(rec_t, dft_rows.T, validity.T).astype(jnp.bfloat16)

    flat = spec.reshape(xs * slots, lanes)
    blocks = lax.axis_size("pair")

    half = lax.broadcasted_iota(jnp.int32, (lanes,), 0) < window_count
    turned = jnp.roll(spec, window_count, axis=-1) * jnp.where(half, 1.0, -1.0).astype(jnp.bfloat16)
    lhs = jnp.stack([spec, turned], axis=0).transpose(2, 0, 1, 3).reshape(slots, 2 * xs, lanes)

    def cross_with(other):
        count = other.shape[0]
        rhs = other.transpose(2, 0, 1, 3).reshape(slots, count * xs, lanes)
        prod = jnp.einsum("fxk,fyk->fxy", lhs, rhs, preferred_element_type=jnp.float32)
        prod = prod.reshape(slots, 2 * comp_count, station_count, count * xs)
        stacked, same = exchange(prod, station_count, bands, band_index)
        per_dev = stacked.shape[3]
        totals = same[0, 0].reshape(per_dev, count, comp_count, station_count)[:, :, 0, :]
        stacked = stacked.reshape(bands, slots, 2 * comp_count, per_dev, count, xs)
        return stacked, totals

    if blocks <= 8 and blocks & (blocks - 1) == 0:
        outs, tots = [], []
        for k in range(blocks):
            held = flat
            if k:
                held = lax.ppermute(flat, "pair", [(p, p ^ k) for p in range(blocks)])
            st, to = cross_with(held.reshape(1, xs, slots, lanes))
            outs.append(st[..., 0, :])
            tots.append(to[:, 0])
        chosen = jnp.take(jnp.stack(outs), round_keys, axis=0, mode="clip")
        totals = jnp.take(jnp.stack(tots), round_keys, axis=0, mode="clip")
        chosen = jnp.moveaxis(chosen, 0, -2)
    else:
        gathered = lax.all_gather(flat, "pair", axis=0, tiled=False)
        partner_list = jnp.bitwise_xor(pair_index, round_keys)
        other = jnp.take(gathered, partner_list, axis=0, mode="clip").reshape(rounds, xs, slots, lanes)
        chosen, totals = cross_with(other)
        totals = totals.transpose(1, 0, 2)
    per_dev = chosen.shape[3]
    stacked = chosen[:, 1:].reshape(
        bands, nb, 2, comp_count, per_dev, rounds, comp_count, station_count
    )

    full_lag = lag_table(sample_points, FREQ, 0, NLAG, FREQ)
    full_lag = full_lag.reshape(2, bands, nb, NLAG).transpose(1, 0, 2, 3)
    lagged = jnp.einsum(
        "gfuairbj,gufl->riabjl",
        stacked,
        full_lag,
        precision=lax.Precision.HIGHEST,
        preferred_element_type=jnp.float32,
    )
    divisor = jnp.maximum(totals, 1.0)[:, :, None, None, :, None]
    lagged = lagged / divisor
    return lagged.reshape(rounds, per_dev, comp_count, comp_count * station_count, NLAG)


def solution(mesh):
    placed = (P(("hours", "win"), None, "pair", None), P(("hours", "win"), "pair"), P())
    return jax.shard_map(
        body,
        mesh=mesh,
        in_specs=placed,
        out_specs=P(None, ("hours", "pair", "win", "band"), None, None, None),
        check_vma=False,
    )
```

```python
import math

import jax
import jax.numpy as jnp
from jax import lax
from jax.experimental import pallas as pl
from jax.experimental.pallas import tpu as pltpu
from jax.sharding import PartitionSpec as P

FREQ = 128
NLAG = 256
ROUNDS = 4
WSTEP = 4


def dft_table(sample_points, bin_count, first_bin):
    sample_moments = jnp.arange(sample_points, dtype=jnp.int32)
    spectral_bin_index = first_bin + 1 + jnp.arange(bin_count, dtype=jnp.int32)
    phase_turns = jnp.mod(sample_moments[:, None] * spectral_bin_index[None, :], sample_points)
    phases = phase_turns.astype(jnp.float32) * (2.0 * math.pi / sample_points)
    hanning_taper = 0.5 - 0.5 * jnp.cos(
        sample_moments.astype(jnp.float32) * (2.0 * math.pi / sample_points)
    )
    weight = (hanning_taper * math.sqrt(8.0 / (3.0 * sample_points)))[:, None]
    return jnp.concatenate([weight * jnp.cos(phases), -(weight * jnp.sin(phases))], axis=1).astype(
        jnp.bfloat16
    )


def lag_table(sample_points, bin_count, first_bin, lag_count, all_bins):
    spectral_bin_index = first_bin + 1 + jnp.arange(bin_count, dtype=jnp.int32)
    shifts = jnp.arange(lag_count, dtype=jnp.int32) - lag_count // 2
    phase_turns = jnp.mod(spectral_bin_index[:, None] * shifts[None, :], sample_points)
    phases = phase_turns.astype(jnp.float32) * (2.0 * math.pi / sample_points)
    lag_scale = 1.0 / math.sqrt(all_bins)
    return jnp.concatenate([jnp.cos(phases) * lag_scale, -(jnp.sin(phases) * lag_scale)], axis=0)


def whiten(spectra, validity):
    bin_count = spectra.shape[-1] // 2
    real_part = spectra[..., :bin_count]
    imag_part = spectra[..., bin_count:]
    band_power = jnp.mean(real_part * real_part + imag_part * imag_part, axis=1)
    amplitude = jnp.sqrt(jnp.maximum(band_power, 0.25))
    factor = validity[:, :, None] / amplitude
    factor = jnp.concatenate([factor, factor], axis=-1)
    return (spectra * factor[:, None]).astype(jnp.bfloat16)


def dft_kernel(rec_ref, table_ref, valid_ref, out_ref):
    station_count, window_count = valid_ref.shape
    comp_count = rec_ref.shape[0] // station_count
    nb = table_ref.shape[0] // 2
    table = table_ref[...]
    zero_row = jnp.zeros((1, window_count), jnp.float32)
    for s in range(station_count):
        parts = []
        for c in range(comp_count):
            z = lax.dot_general(
                table,
                rec_ref[c * station_count + s],
                (((1,), (1,)), ((), ())),
                preferred_element_type=jnp.float32,
            )
            parts.append((z[:nb], z[nb:]))
        total = parts[0][0] * parts[0][0] + parts[0][1] * parts[0][1]
        for c in range(1, comp_count):
            total = total + (parts[c][0] * parts[c][0] + parts[c][1] * parts[c][1])
        band_power = total / float(comp_count)
        amplitude = jnp.sqrt(jnp.maximum(band_power, 0.25))
        valid_row = valid_ref[pl.ds(s, 1), :]
        factor = valid_row / amplitude
        for c in range(comp_count):
            x = c * station_count + s
            out_ref[x, pl.ds(0, 1), pl.ds(0, window_count)] = valid_row if c == 0 else zero_row
            out_ref[x, pl.ds(0, 1), pl.ds(window_count, window_count)] = zero_row
            out_ref[x, pl.ds(1, nb), pl.ds(0, window_count)] = parts[c][0] * factor
            out_ref[x, pl.ds(1, nb), pl.ds(window_count, window_count)] = parts[c][1] * factor


def dft_whiten(rec_t, table_t, valid_t):
    rows, window_count, sample_points = rec_t.shape
    nb = table_t.shape[0] // 2
    return pl.pallas_call(
        dft_kernel,
        out_shape=jax.ShapeDtypeStruct((rows, 1 + nb, 2 * window_count), jnp.float32),
        cost_estimate=pl.CostEstimate(
            flops=2 * rows * window_count * sample_points * 2 * nb,
            transcendentals=rows * nb * window_count,
            bytes_accessed=2 * rec_t.size + 2 * table_t.size + 4 * rows * (nb + 1) * 2 * window_count,
        ),
    )(rec_t, table_t, valid_t)


def exchange(prod, station_count, bands, band_index):
    group = lax.axis_size("win") * bands
    per_dev = station_count // group
    me = lax.axis_index("win") * bands + band_index
    by_offset = [None] * bands
    for shift in range(group):
        dest = (me + shift) % group
        chunk = lax.dynamic_slice_in_dim(prod, dest * per_dev, per_dev, 2)
        if shift:
            perm = [(k, (k + shift) % group) for k in range(group)]
            chunk = lax.ppermute(chunk.astype(jnp.bfloat16), ("win", "band"), perm)
            chunk = chunk.astype(jnp.float32)
        q = shift % bands
        by_offset[q] = chunk if by_offset[q] is None else by_offset[q] + chunk
    ordered = []
    for bb in range(bands):
        pick = by_offset[0]
        for q in range(1, bands):
            pick = jnp.where((band_index - q) % bands == bb, by_offset[q], pick)
        ordered.append(pick)
    return jnp.stack(ordered, axis=0), by_offset[0]


def body(records, valid_mask, round_keys):
    window_count, comp_count, station_count, sample_points = records.shape
    bands = lax.axis_size("band")
    band_index = lax.axis_index("band")
    pair_index = lax.axis_index("pair")
    nb = FREQ // bands
    rounds = round_keys.shape[0]
    xs = comp_count * station_count
    lanes = 2 * window_count
    slots = nb + 1

    dft_rows = dft_table(sample_points, nb, band_index * nb)
    rec_t = records.reshape(window_count, xs, sample_points).transpose(1, 0, 2)
    validity = valid_mask.astype(jnp.float32)
    spec = dft_whiten(rec_t, dft_rows.T, validity.T).astype(jnp.bfloat16)

    flat = spec.reshape(xs * slots, lanes)
    blocks = lax.axis_size("pair")

    half = lax.broadcasted_iota(jnp.int32, (lanes,), 0) < window_count
    turned = jnp.roll(spec, window_count, axis=-1) * jnp.where(half, 1.0, -1.0).astype(jnp.bfloat16)
    lhs = jnp.stack([spec, turned], axis=0).transpose(2, 0, 1, 3).reshape(slots, 2 * xs, lanes)

    def cross_with(other):
        count = other.shape[0]
        rhs = other.transpose(2, 0, 1, 3).reshape(slots, count * xs, lanes)
        prod = jnp.einsum("fxk,fyk->fxy", lhs, rhs, preferred_element_type=jnp.float32)
        prod = prod.reshape(slots, 2 * comp_count, station_count, count * xs)
        stacked, same = exchange(prod, station_count, bands, band_index)
        per_dev = stacked.shape[3]
        totals = same[0, 0].reshape(per_dev, count, comp_count, station_count)[:, :, 0, :]
        stacked = stacked.reshape(bands, slots, 2 * comp_count, per_dev, count, xs)
        return stacked, totals

    full_lag = lag_table(sample_points, FREQ, 0, NLAG, FREQ)
    full_lag = full_lag.reshape(2, bands, nb, NLAG).transpose(1, 0, 2, 3)

    def to_lags(chosen, subscripts):
        per_dev = chosen.shape[3]
        shape = chosen.shape[:3] + (per_dev,) + chosen.shape[4:-1] + (comp_count, station_count)
        stacked = chosen[:, 1:].reshape((bands, nb, 2, comp_count) + shape[3:])
        return jnp.einsum(
            subscripts,
            stacked,
            full_lag,
            precision=lax.Precision.HIGHEST,
            preferred_element_type=jnp.float32,
        )

    if blocks <= 8 and blocks & (blocks - 1) == 0:
        lags, tots = [], []
        for k in range(blocks):
            held = flat
            if k:
                held = lax.ppermute(flat, "pair", [(p, p ^ k) for p in range(blocks)])
            st, to = cross_with(held.reshape(1, xs, slots, lanes))
            lags.append(to_lags(st[..., 0, :], "gfuaibj,gufl->iabjl"))
            tots.append(to[:, 0])
        lagged = jnp.take(jnp.stack(lags), round_keys, axis=0, mode="clip")
        totals = jnp.take(jnp.stack(tots), round_keys, axis=0, mode="clip")
    else:
        gathered = lax.all_gather(flat, "pair", axis=0, tiled=False)
        partner_list = jnp.bitwise_xor(pair_index, round_keys)
        other = jnp.take(gathered, partner_list, axis=0, mode="clip").reshape(rounds, xs, slots, lanes)
        chosen, totals = cross_with(other)
        totals = totals.transpose(1, 0, 2)
        lagged = to_lags(chosen, "gfuairbj,gufl->riabjl")
    per_dev = lagged.shape[1]
    divisor = jnp.maximum(totals, 1.0)[:, :, None, None, :, None]
    lagged = lagged / divisor
    return lagged.reshape(rounds, per_dev, comp_count, comp_count * station_count, NLAG)


def solution(mesh):
    placed = (P(("hours", "win"), None, "pair", None), P(("hours", "win"), "pair"), P())
    return jax.shard_map(
        body,
        mesh=mesh,
        in_specs=placed,
        out_specs=P(None, ("hours", "pair", "win", "band"), None, None, None),
        check_vma=False,
    )
```

```python
import math

import jax
import jax.numpy as jnp
from jax import lax
from jax.experimental import pallas as pl
from jax.experimental.pallas import tpu as pltpu
from jax.sharding import PartitionSpec as P

FREQ = 128
NLAG = 256
ROUNDS = 4
WSTEP = 4


def dft_table(sample_points, bin_count, first_bin):
    sample_moments = jnp.arange(sample_points, dtype=jnp.int32)
    spectral_bin_index = first_bin + 1 + jnp.arange(bin_count, dtype=jnp.int32)
    phase_turns = jnp.mod(sample_moments[:, None] * spectral_bin_index[None, :], sample_points)
    phases = phase_turns.astype(jnp.float32) * (2.0 * math.pi / sample_points)
    hanning_taper = 0.5 - 0.5 * jnp.cos(
        sample_moments.astype(jnp.float32) * (2.0 * math.pi / sample_points)
    )
    weight = (hanning_taper * math.sqrt(8.0 / (3.0 * sample_points)))[:, None]
    return jnp.concatenate([weight * jnp.cos(phases), -(weight * jnp.sin(phases))], axis=1).astype(
        jnp.bfloat16
    )


def lag_table(sample_points, bin_count, first_bin, lag_count, all_bins):
    spectral_bin_index = first_bin + 1 + jnp.arange(bin_count, dtype=jnp.int32)
    shifts = jnp.arange(lag_count, dtype=jnp.int32) - lag_count // 2
    phase_turns = jnp.mod(spectral_bin_index[:, None] * shifts[None, :], sample_points)
    phases = phase_turns.astype(jnp.float32) * (2.0 * math.pi / sample_points)
    lag_scale = 1.0 / math.sqrt(all_bins)
    return jnp.concatenate([jnp.cos(phases) * lag_scale, -(jnp.sin(phases) * lag_scale)], axis=0)


def whiten(spectra, validity):
    bin_count = spectra.shape[-1] // 2
    real_part = spectra[..., :bin_count]
    imag_part = spectra[..., bin_count:]
    band_power = jnp.mean(real_part * real_part + imag_part * imag_part, axis=1)
    amplitude = jnp.sqrt(jnp.maximum(band_power, 0.25))
    factor = validity[:, :, None] / amplitude
    factor = jnp.concatenate([factor, factor], axis=-1)
    return (spectra * factor[:, None]).astype(jnp.bfloat16)


def dft_kernel(rec_ref, table_ref, valid_ref, out_ref):
    station_count, window_count = valid_ref.shape
    comp_count = rec_ref.shape[0] // station_count
    nb = table_ref.shape[0] // 2
    table = table_ref[...]
    zero_row = jnp.zeros((1, window_count), jnp.float32)
    for s in range(station_count):
        parts = []
        for c in range(comp_count):
            z = lax.dot_general(
                table,
                rec_ref[c * station_count + s],
                (((1,), (1,)), ((), ())),
                preferred_element_type=jnp.float32,
            )
            parts.append((z[:nb], z[nb:]))
        total = parts[0][0] * parts[0][0] + parts[0][1] * parts[0][1]
        for c in range(1, comp_count):
            total = total + (parts[c][0] * parts[c][0] + parts[c][1] * parts[c][1])
        band_power = total / float(comp_count)
        amplitude = jnp.sqrt(jnp.maximum(band_power, 0.25))
        valid_row = valid_ref[pl.ds(s, 1), :]
        factor = valid_row / amplitude
        for c in range(comp_count):
            x = c * station_count + s
            out_ref[x, pl.ds(0, 1), pl.ds(0, window_count)] = valid_row if c == 0 else zero_row
            out_ref[x, pl.ds(0, 1), pl.ds(window_count, window_count)] = zero_row
            out_ref[x, pl.ds(1, nb), pl.ds(0, window_count)] = parts[c][0] * factor
            out_ref[x, pl.ds(1, nb), pl.ds(window_count, window_count)] = parts[c][1] * factor


def dft_whiten(rec_t, table_t, valid_t):
    rows, window_count, sample_points = rec_t.shape
    nb = table_t.shape[0] // 2
    return pl.pallas_call(
        dft_kernel,
        out_shape=jax.ShapeDtypeStruct((rows, 1 + nb, 2 * window_count), jnp.float32),
        cost_estimate=pl.CostEstimate(
            flops=2 * rows * window_count * sample_points * 2 * nb,
            transcendentals=rows * nb * window_count,
            bytes_accessed=2 * rec_t.size + 2 * table_t.size + 4 * rows * (nb + 1) * 2 * window_count,
        ),
    )(rec_t, table_t, valid_t)


def exchange(prod, station_count, bands, band_index):
    group = lax.axis_size("win") * bands
    per_dev = station_count // group
    me = lax.axis_index("win") * bands + band_index
    by_offset = [None] * bands
    for shift in range(group):
        dest = (me + shift) % group
        chunk = lax.dynamic_slice_in_dim(prod, dest * per_dev, per_dev, 2)
        if shift:
            perm = [(k, (k + shift) % group) for k in range(group)]
            chunk = lax.ppermute(chunk.astype(jnp.bfloat16), ("win", "band"), perm)
            chunk = chunk.astype(jnp.float32)
        q = shift % bands
        by_offset[q] = chunk if by_offset[q] is None else by_offset[q] + chunk
    ordered = []
    for bb in range(bands):
        pick = by_offset[0]
        for q in range(1, bands):
            pick = jnp.where((band_index - q) % bands == bb, by_offset[q], pick)
        ordered.append(pick)
    return jnp.stack(ordered, axis=0), by_offset[0]


def body(records, valid_mask, round_keys):
    window_count, comp_count, station_count, sample_points = records.shape
    bands = lax.axis_size("band")
    band_index = lax.axis_index("band")
    pair_index = lax.axis_index("pair")
    nb = FREQ // bands
    rounds = round_keys.shape[0]
    xs = comp_count * station_count
    lanes = 2 * window_count
    slots = nb + 1

    dft_rows = dft_table(sample_points, nb, band_index * nb)
    rec_t = records.reshape(window_count, xs, sample_points).transpose(1, 0, 2)
    validity = valid_mask.astype(jnp.float32)
    spec = dft_whiten(rec_t, dft_rows.T, validity.T).astype(jnp.bfloat16)

    flat = spec.reshape(xs * slots, lanes)
    blocks = lax.axis_size("pair")

    half = lax.broadcasted_iota(jnp.int32, (lanes,), 0) < window_count
    turned = jnp.roll(spec, window_count, axis=-1) * jnp.where(half, 1.0, -1.0).astype(jnp.bfloat16)
    lhs = jnp.stack([spec, turned], axis=0).transpose(2, 0, 1, 3).reshape(slots, 2 * xs, lanes)

    def cross_with(other):
        count = other.shape[0]
        rhs = other.transpose(2, 0, 1, 3).reshape(slots, count * xs, lanes)
        prod = jnp.einsum("fxk,fyk->fxy", lhs, rhs, preferred_element_type=jnp.float32)
        prod = prod.reshape(slots, 2 * comp_count, station_count, count * xs)
        stacked, same = exchange(prod, station_count, bands, band_index)
        per_dev = stacked.shape[3]
        totals = same[0, 0].reshape(per_dev, count, comp_count, station_count)[:, :, 0, :]
        stacked = stacked.reshape(bands, slots, 2 * comp_count, per_dev, count, xs)
        return stacked, totals

    full_lag = lag_table(sample_points, FREQ, 0, NLAG, FREQ)
    full_lag = full_lag.reshape(2, bands, nb, NLAG).transpose(1, 0, 2, 3)

    def to_lags(chosen, subscripts):
        per_dev = chosen.shape[3]
        shape = chosen.shape[:3] + (per_dev,) + chosen.shape[4:-1] + (comp_count, station_count)
        stacked = chosen[:, 1:].reshape((bands, nb, 2, comp_count) + shape[3:])
        return jnp.einsum(
            subscripts,
            stacked,
            full_lag,
            precision=lax.Precision.HIGHEST,
            preferred_element_type=jnp.float32,
        )

    if blocks <= 8 and blocks & (blocks - 1) == 0:
        held = [flat] + [
            lax.ppermute(flat, "pair", [(p, p ^ k) for p in range(blocks)]) for k in range(1, blocks)
        ]
        groups = [[0, 1]] + [[k] for k in range(2, blocks)]
        lags, tots = [], []
        for members in groups:
            other = jnp.stack([held[k] for k in members]).reshape(len(members), xs, slots, lanes)
            st, to = cross_with(other)
            for n in range(len(members)):
                lags.append(to_lags(st[..., n, :], "gfuaibj,gufl->iabjl"))
                tots.append(to[:, n])
        lagged = jnp.take(jnp.stack(lags), round_keys, axis=0, mode="clip")
        totals = jnp.take(jnp.stack(tots), round_keys, axis=0, mode="clip")
    else:
        gathered = lax.all_gather(flat, "pair", axis=0, tiled=False)
        partner_list = jnp.bitwise_xor(pair_index, round_keys)
        other = jnp.take(gathered, partner_list, axis=0, mode="clip").reshape(rounds, xs, slots, lanes)
        chosen, totals = cross_with(other)
        totals = totals.transpose(1, 0, 2)
        lagged = to_lags(chosen, "gfuairbj,gufl->riabjl")
    per_dev = lagged.shape[1]
    divisor = jnp.maximum(totals, 1.0)[:, :, None, None, :, None]
    lagged = lagged / divisor
    return lagged.reshape(rounds, per_dev, comp_count, comp_count * station_count, NLAG)


def solution(mesh):
    placed = (P(("hours", "win"), None, "pair", None), P(("hours", "win"), "pair"), P())
    return jax.shard_map(
        body,
        mesh=mesh,
        in_specs=placed,
        out_specs=P(None, ("hours", "pair", "win", "band"), None, None, None),
        check_vma=False,
    )
```

```python
import math

import jax
import jax.numpy as jnp
from jax import lax
from jax.experimental import pallas as pl
from jax.experimental.pallas import tpu as pltpu
from jax.sharding import PartitionSpec as P

FREQ = 128
NLAG = 256
ROUNDS = 4
WSTEP = 4


def dft_table(sample_points, bin_count, first_bin):
    sample_moments = jnp.arange(sample_points, dtype=jnp.int32)
    spectral_bin_index = first_bin + 1 + jnp.arange(bin_count, dtype=jnp.int32)
    phase_turns = jnp.mod(sample_moments[:, None] * spectral_bin_index[None, :], sample_points)
    phases = phase_turns.astype(jnp.float32) * (2.0 * math.pi / sample_points)
    hanning_taper = 0.5 - 0.5 * jnp.cos(
        sample_moments.astype(jnp.float32) * (2.0 * math.pi / sample_points)
    )
    weight = (hanning_taper * math.sqrt(8.0 / (3.0 * sample_points)))[:, None]
    return jnp.concatenate([weight * jnp.cos(phases), -(weight * jnp.sin(phases))], axis=1).astype(
        jnp.bfloat16
    )


def lag_table(sample_points, bin_count, first_bin, lag_count, all_bins):
    spectral_bin_index = first_bin + 1 + jnp.arange(bin_count, dtype=jnp.int32)
    shifts = jnp.arange(lag_count, dtype=jnp.int32) - lag_count // 2
    phase_turns = jnp.mod(spectral_bin_index[:, None] * shifts[None, :], sample_points)
    phases = phase_turns.astype(jnp.float32) * (2.0 * math.pi / sample_points)
    lag_scale = 1.0 / math.sqrt(all_bins)
    return jnp.concatenate([jnp.cos(phases) * lag_scale, -(jnp.sin(phases) * lag_scale)], axis=0)


def whiten(spectra, validity):
    bin_count = spectra.shape[-1] // 2
    real_part = spectra[..., :bin_count]
    imag_part = spectra[..., bin_count:]
    band_power = jnp.mean(real_part * real_part + imag_part * imag_part, axis=1)
    amplitude = jnp.sqrt(jnp.maximum(band_power, 0.25))
    factor = validity[:, :, None] / amplitude
    factor = jnp.concatenate([factor, factor], axis=-1)
    return (spectra * factor[:, None]).astype(jnp.bfloat16)


def dft_kernel(rec_ref, table_ref, valid_ref, out_ref):
    station_count, window_count = valid_ref.shape
    comp_count = rec_ref.shape[0] // station_count
    nb = table_ref.shape[0] // 2
    table = table_ref[...]
    zero_row = jnp.zeros((1, window_count), jnp.float32)
    for s in range(station_count):
        parts = []
        for c in range(comp_count):
            z = lax.dot_general(
                table,
                rec_ref[c * station_count + s],
                (((1,), (1,)), ((), ())),
                preferred_element_type=jnp.float32,
            )
            parts.append((z[:nb], z[nb:]))
        total = parts[0][0] * parts[0][0] + parts[0][1] * parts[0][1]
        for c in range(1, comp_count):
            total = total + (parts[c][0] * parts[c][0] + parts[c][1] * parts[c][1])
        band_power = total / float(comp_count)
        amplitude = jnp.sqrt(jnp.maximum(band_power, 0.25))
        valid_row = valid_ref[pl.ds(s, 1), :]
        factor = valid_row / amplitude
        for c in range(comp_count):
            x = c * station_count + s
            head = jnp.concatenate([valid_row if c == 0 else zero_row, parts[c][0] * factor], axis=0)
            tail = jnp.concatenate([zero_row, parts[c][1] * factor], axis=0)
            out_ref[x, :, pl.ds(0, window_count)] = head.astype(out_ref.dtype)
            out_ref[x, :, pl.ds(window_count, window_count)] = tail.astype(out_ref.dtype)


def dft_whiten(rec_t, table_t, valid_t):
    rows, window_count, sample_points = rec_t.shape
    nb = table_t.shape[0] // 2
    return pl.pallas_call(
        dft_kernel,
        out_shape=jax.ShapeDtypeStruct((rows, 1 + nb, 2 * window_count), jnp.bfloat16),
        cost_estimate=pl.CostEstimate(
            flops=2 * rows * window_count * sample_points * 2 * nb,
            transcendentals=rows * nb * window_count,
            bytes_accessed=2 * rec_t.size + 2 * table_t.size + 4 * rows * (nb + 1) * 2 * window_count,
        ),
    )(rec_t, table_t, valid_t)


def exchange(prod, station_count, bands, band_index):
    group = lax.axis_size("win") * bands
    per_dev = station_count // group
    me = lax.axis_index("win") * bands + band_index
    by_offset = [None] * bands
    for shift in range(group):
        dest = (me + shift) % group
        chunk = lax.dynamic_slice_in_dim(prod, dest * per_dev, per_dev, 2)
        if shift:
            perm = [(k, (k + shift) % group) for k in range(group)]
            chunk = lax.ppermute(chunk.astype(jnp.bfloat16), ("win", "band"), perm)
            chunk = chunk.astype(jnp.float32)
        q = shift % bands
        by_offset[q] = chunk if by_offset[q] is None else by_offset[q] + chunk
    ordered = []
    for bb in range(bands):
        pick = by_offset[0]
        for q in range(1, bands):
            pick = jnp.where((band_index - q) % bands == bb, by_offset[q], pick)
        ordered.append(pick)
    return jnp.stack(ordered, axis=0), by_offset[0]


def body(records, valid_mask, round_keys):
    window_count, comp_count, station_count, sample_points = records.shape
    bands = lax.axis_size("band")
    band_index = lax.axis_index("band")
    pair_index = lax.axis_index("pair")
    nb = FREQ // bands
    rounds = round_keys.shape[0]
    xs = comp_count * station_count
    lanes = 2 * window_count
    slots = nb + 1

    dft_rows = dft_table(sample_points, nb, band_index * nb)
    rec_t = records.reshape(window_count, xs, sample_points).transpose(1, 0, 2)
    validity = valid_mask.astype(jnp.float32)
    spec = dft_whiten(rec_t, dft_rows.T, validity.T)

    flat = spec.reshape(xs * slots, lanes)
    blocks = lax.axis_size("pair")

    half = lax.broadcasted_iota(jnp.int32, (lanes,), 0) < window_count
    turned = jnp.roll(spec, window_count, axis=-1) * jnp.where(half, 1.0, -1.0).astype(jnp.bfloat16)
    lhs = jnp.stack([spec, turned], axis=0).transpose(2, 0, 1, 3).reshape(slots, 2 * xs, lanes)

    def cross_with(other):
        count = other.shape[0]
        rhs = other.transpose(2, 0, 1, 3).reshape(slots, count * xs, lanes)
        prod = jnp.einsum("fxk,fyk->fxy", lhs, rhs, preferred_element_type=jnp.float32)
        prod = prod.reshape(slots, 2 * comp_count, station_count, count * xs)
        stacked, same = exchange(prod, station_count, bands, band_index)
        per_dev = stacked.shape[3]
        totals = same[0, 0].reshape(per_dev, count, comp_count, station_count)[:, :, 0, :]
        stacked = stacked.reshape(bands, slots, 2 * comp_count, per_dev, count, xs)
        return stacked, totals

    full_lag = lag_table(sample_points, FREQ, 0, NLAG, FREQ)
    full_lag = full_lag.reshape(2, bands, nb, NLAG).transpose(1, 0, 2, 3)

    def to_lags(chosen, subscripts):
        per_dev = chosen.shape[3]
        shape = chosen.shape[:3] + (per_dev,) + chosen.shape[4:-1] + (comp_count, station_count)
        stacked = chosen[:, 1:].reshape((bands, nb, 2, comp_count) + shape[3:])
        return jnp.einsum(
            subscripts,
            stacked,
            full_lag,
            precision=lax.Precision.HIGHEST,
            preferred_element_type=jnp.float32,
        )

    if blocks <= 8 and blocks & (blocks - 1) == 0:
        lags, tots = [], []
        for k in range(blocks):
            held = flat
            if k:
                held = lax.ppermute(flat, "pair", [(p, p ^ k) for p in range(blocks)])
            st, to = cross_with(held.reshape(1, xs, slots, lanes))
            lags.append(to_lags(st[..., 0, :], "gfuaibj,gufl->iabjl"))
            tots.append(to[:, 0])
        lagged = jnp.take(jnp.stack(lags), round_keys, axis=0, mode="clip")
        totals = jnp.take(jnp.stack(tots), round_keys, axis=0, mode="clip")
    else:
        gathered = lax.all_gather(flat, "pair", axis=0, tiled=False)
        partner_list = jnp.bitwise_xor(pair_index, round_keys)
        other = jnp.take(gathered, partner_list, axis=0, mode="clip").reshape(rounds, xs, slots, lanes)
        chosen, totals = cross_with(other)
        totals = totals.transpose(1, 0, 2)
        lagged = to_lags(chosen, "gfuairbj,gufl->riabjl")
    per_dev = lagged.shape[1]
    divisor = jnp.maximum(totals, 1.0)[:, :, None, None, :, None]
    lagged = lagged / divisor
    return lagged.reshape(rounds, per_dev, comp_count, comp_count * station_count, NLAG)


def solution(mesh):
    placed = (P(("hours", "win"), None, "pair", None), P(("hours", "win"), "pair"), P())
    return jax.shard_map(
        body,
        mesh=mesh,
        in_specs=placed,
        out_specs=P(None, ("hours", "pair", "win", "band"), None, None, None),
        check_vma=False,
    )
```
